512 devices in a mesh: cuts: 16 (over z_lo, core), stem: 32 (over z_hi, x, y).
Axes of the slice: x: 4, y: 4, z: 16 (z_hi: 2, z_lo: 8; z = z_hi * 8 + z_lo), core: 2. Of those that a mesh axis runs over, the one named last changes fastest.
Arguments:
- stem_tensor: bfloat16 [32, 16384, 2, 512], P('cuts', 'stem'), may hold values from -6 to 6
- branch_tensor: bfloat16 [32, 512, 2, 512], P('cuts', 'stem'), may hold values from -0.1875 to 0.1875
- open_tensor: bfloat16 [32, 16384, 2, 512], P('cuts', 'stem'), may hold values from -0.75 to 0.75
- open_order: int32 [32, 512], P('cuts'), may hold values from 0 to 511, each once within a row
Outputs:
- amplitudes: float32 [32, 512, 2, 512], P('stem', 'cuts')
The draws below stay inside these ranges and needn't reach their ends.
Inputs may be any that keep to these rules, and one draw needn't show every extreme that they name: Each row of open_order holds every number of 0 to 511 once.
All inputs are finite; a program needn't handle non-finite values.
Results may differ from the reference program's by a relative error of at most 0.0003.
Values may be sent and summed in bfloat16 or wider, within the bound.
No kernel may reach another device: no remote copies, remote signals or barrier semaphores. Data moves between devices by JAX's collectives and lax.ppermute only.
A program may use at most 64 MiB of HBM per device.

```python
import jax
import jax.numpy as jnp
from jax import lax

K = 512
M_DEV = 512
SLICES = 32
GROUPS = 32
M = 16384


def shard_levels(own_key, shape, cuts, low, high):
    def one(axis_at, shards_of):
        steps = jax.random.uniform(jax.random.fold_in(jax.random.fold_in(own_key, 6), axis_at), (shards_of,), jnp.float32, low / len(cuts), high / len(cuts))
        return jnp.repeat(jnp.exp(steps), shape[axis_at] // shards_of).reshape((-1,) + (1,) * (len(shape) - axis_at - 1))

    loudness = one(*cuts[0])
    for cut in cuts[1:]:
        loudness = loudness * one(*cut)
    return loudness


def scatter_about(key, dims, spread, reach, pieces=(), held_as=jnp.bfloat16):
    values = spread * jax.random.normal(key, dims, jnp.float32)
    if pieces:
        values = values * shard_levels(key, dims, pieces, -0.22, 0.18)
    return jnp.clip(values, -reach, reach).astype(held_as)


def setup_inputs(seed: int = 0) -> dict:
    arg_keys = jax.random.split(jax.random.key(seed), 5)
    return {
        "stem_tensor": scatter_about(arg_keys[0], (SLICES, M, 2, K), 1.0, 6.0, ((0, 16), (1, 32))),
        "branch_tensor": scatter_about(arg_keys[1], (SLICES, K, 2, K), (2 * K) ** -0.5, 0.1875, ((0, 16), (1, 32))),
        "open_tensor": scatter_about(arg_keys[2], (SLICES, M, 2, K), (2 * SLICES) ** -0.5, 0.75, ((0, 16), (1, 32))),
        "open_order": jax.vmap(lambda own: jax.random.permutation(own, K))(jax.random.split(arg_keys[3], SLICES)).reshape((SLICES, K)).astype(jnp.int32),
    }


def expand_branch(branch_block):
    top_rows = jnp.concatenate([branch_block[:, 0, :], branch_block[:, 1, :]], axis=1)
    bottom_rows = jnp.concatenate([-branch_block[:, 1, :], branch_block[:, 0, :]], axis=1)
    return jnp.concatenate([top_rows, bottom_rows], axis=0)


def reference(stem_tensor, branch_tensor, open_tensor, open_order):
    def accumulate(summed, inputs):
        stem_block, branch_block, open_block, order_block = inputs
        stem_cols = stem_block.reshape(stem_block.shape[0], 2 * K)
        stem_image = jnp.dot(stem_cols, expand_branch(branch_block), preferred_element_type=jnp.float32)
        stem_image = stem_image.reshape(stem_block.shape[0], 2, K)
        placed = jnp.take(stem_image, order_block.astype(jnp.int32), axis=2)
        opened = open_block.astype(jnp.float32)
        real_part = placed[:, 0, :] * opened[:, 0, :] - placed[:, 1, :] * opened[:, 1, :]
        imag_part = placed[:, 0, :] * opened[:, 1, :] + placed[:, 1, :] * opened[:, 0, :]
        return summed + jnp.stack([real_part, imag_part], axis=1), None

    initial = jnp.zeros((M, 2, K), jnp.float32)
    summed, unused = lax.scan(accumulate, initial, (stem_tensor, branch_tensor, open_tensor, open_order))
    return summed.reshape(GROUPS, M_DEV, 2, K)
```

```python
import jax
import jax.numpy as jnp
from jax import lax
from jax.sharding import Mesh
from jax.sharding import PartitionSpec as P

CUTS = ("zl", "core")
STEM = ("zh", "x", "y")


def split_mesh(mesh):
    devices = mesh.devices.reshape(8, 2, 2, 4, 4)
    return Mesh(devices, CUTS + STEM)


def expand_branch(block):
    top_rows = jnp.concatenate([block[:, 0, :], block[:, 1, :]], axis=-1)
    bottom_rows = jnp.concatenate([-block[:, 1, :], block[:, 0, :]], axis=-1)
    return jnp.concatenate([top_rows, bottom_rows], axis=0)


def body(stem_tensor, branch_tensor, open_tensor, open_order):
    slice_count, row_count, _, width = stem_tensor.shape
    permuted = jnp.stack(
        [jnp.take(branch_tensor[t], open_order[t], axis=-1) for t in range(slice_count)]
    )
    pair = lax.all_gather(permuted, "zh", axis=1, tiled=False)
    gathered = lax.all_gather(pair, ("x", "y"), axis=1, tiled=False)
    gathered = jnp.swapaxes(gathered, 1, 2).reshape(slice_count, -1, 2, width)
    local_sum = None
    for t in range(slice_count):
        stem_cols = stem_tensor[t].reshape(row_count, 2 * width)
        placed = jnp.dot(stem_cols, expand_branch(gathered[t]), preferred_element_type=jnp.float32)
        placed = placed.reshape(row_count, 2, width)
        opened = open_tensor[t].astype(jnp.float32)
        real_part = placed[:, 0, :] * opened[:, 0, :] - placed[:, 1, :] * opened[:, 1, :]
        imag_part = placed[:, 0, :] * opened[:, 1, :] + placed[:, 1, :] * opened[:, 0, :]
        term = jnp.stack([real_part, imag_part], axis=1)
        local_sum = term if local_sum is None else local_sum + term
    zl_count = lax.axis_size("zl")
    core_count = lax.axis_size("core")
    block_rows = row_count // (zl_count * core_count)
    shaped = local_sum.reshape(zl_count, core_count, block_rows, 2, width)
    shaped = lax.psum_scatter(shaped, "core", scatter_dimension=1, tiled=True)
    shaped = lax.psum_scatter(shaped, "zl", scatter_dimension=0, tiled=True)
    return shaped.reshape(1, block_rows, 2, width)


def solution(mesh):
    fine = split_mesh(mesh)
    spec = P(CUTS, STEM, None, None)
    return jax.shard_map(
        body,
        mesh=fine,
        in_specs=(spec, spec, spec, P(CUTS, None)),
        out_specs=P(STEM, CUTS, None, None),
        check_vma=False,
    )
```

```python
import jax
import jax.numpy as jnp
import numpy as np
from jax import lax
from jax.sharding import Mesh
from jax.sharding import PartitionSpec as P

CUTS = ("zl", "core")
STEM = ("zh", "x", "y")
FOLDED = (0, 2, 4, 6, 7, 5, 3, 1)


def split_mesh(mesh):
    devices = mesh.devices.reshape(8, 2, 2, 4, 4)
    return Mesh(devices, CUTS + STEM)


def expand_branch(block):
    top_rows = jnp.concatenate([block[:, 0, :], block[:, 1, :]], axis=-1)
    bottom_rows = jnp.concatenate([-block[:, 1, :], block[:, 0, :]], axis=-1)
    return jnp.concatenate([top_rows, bottom_rows], axis=0)


def shift_pairs(count, step):
    return [(i, (i + step) % count) for i in range(count)]


def ring_gather(block, axis):
    count = lax.axis_size(axis)
    me = lax.axis_index(axis)
    from_left = lax.ppermute(block, axis, shift_pairs(count, 1))
    from_right = lax.ppermute(block, axis, shift_pairs(count, -1))
    half = block.shape[-1] // 2
    far_a = lax.ppermute(from_left[..., :half], axis, shift_pairs(count, 1))
    far_b = lax.ppermute(from_right[..., half:], axis, shift_pairs(count, -1))
    far = jnp.concatenate([far_a, far_b], axis=-1)
    relative = jnp.stack([block, from_right, far, from_left])
    return jnp.roll(relative, me, axis=0)


def zl_ring_scatter(blocks):
    count = len(FOLDED)
    position_of = np.zeros(count, np.int32)
    for pos, chip in enumerate(FOLDED):
        position_of[chip] = pos
    chips = jnp.asarray(np.array(FOLDED, np.int32))
    pos = jnp.asarray(position_of)[lax.axis_index("zl")]
    pairs = [(FOLDED[i], FOLDED[(i + 1) % count]) for i in range(count)]

    def own(step):
        chip = chips[(pos - step - 1) % count]
        return lax.dynamic_index_in_dim(blocks, chip, 0, keepdims=False)

    running = own(0)
    for step in range(1, count):
        running = lax.ppermute(running, "zl", pairs) + own(step)
    return running


def body(stem_tensor, branch_tensor, open_tensor, open_order):
    slice_count, row_count, _, width = stem_tensor.shape
    permuted = jnp.stack(
        [jnp.take(branch_tensor[t], open_order[t], axis=-1) for t in range(slice_count)]
    )
    other = lax.ppermute(permuted, "zh", shift_pairs(2, 1))
    low = lax.axis_index("zh") == 0
    pair = jnp.where(low, jnp.stack([permuted, other], axis=1), jnp.stack([other, permuted], axis=1))
    gathered = ring_gather(pair, "y")
    gathered = ring_gather(gathered, "x")
    gathered = jnp.transpose(gathered, (2, 3, 0, 1, 4, 5, 6)).reshape(slice_count, -1, 2, width)
    local_sum = None
    for t in range(slice_count):
        stem_cols = stem_tensor[t].reshape(row_count, 2 * width)
        placed = jnp.dot(stem_cols, expand_branch(gathered[t]), preferred_element_type=jnp.float32)
        placed = placed.reshape(row_count, 2, width)
        opened = open_tensor[t].astype(jnp.float32)
        real_part = placed[:, 0, :] * opened[:, 0, :] - placed[:, 1, :] * opened[:, 1, :]
        imag_part = placed[:, 0, :] * opened[:, 1, :] + placed[:, 1, :] * opened[:, 0, :]
        term = jnp.stack([real_part, imag_part], axis=1)
        local_sum = term if local_sum is None else local_sum + term
    zl_count = lax.axis_size("zl")
    block_rows = row_count // (zl_count * 2)
    shaped = local_sum.reshape(zl_count, 2, block_rows, 2, width)
    core = lax.axis_index("core")
    mine = lax.dynamic_index_in_dim(shaped, core, 1, keepdims=False)
    theirs = lax.dynamic_index_in_dim(shaped, 1 - core, 1, keepdims=False)
    mine = mine + lax.ppermute(theirs, "core", shift_pairs(2, 1))
    result = zl_ring_scatter(mine)
    return result.reshape(1, block_rows, 2, width)


def solution(mesh):
    fine = split_mesh(mesh)
    spec = P(CUTS, STEM, None, None)
    return jax.shard_map(
        body,
        mesh=fine,
        in_specs=(spec, spec, spec, P(CUTS, None)),
        out_specs=P(STEM, CUTS, None, None),
        check_vma=False,
    )
```

```python
import jax
import jax.numpy as jnp
from jax import lax
from jax.experimental import pallas as pl
from jax.sharding import Mesh
from jax.sharding import PartitionSpec as P

CUTS = ("zl", "core")
STEM = ("zh", "x", "y")
ROW_TILE = 256


def split_mesh(mesh):
    devices = mesh.devices.reshape(8, 2, 2, 4, 4)
    return Mesh(devices, CUTS + STEM)


def shift_pairs(count, step):
    return [(i, (i + step) % count) for i in range(count)]


def ring_gather(block, axis, along):
    count = lax.axis_size(axis)
    me = lax.axis_index(axis)
    from_left = lax.ppermute(block, axis, shift_pairs(count, 1))
    from_right = lax.ppermute(block, axis, shift_pairs(count, -1))
    half = block.shape[-1] // 2
    far_a = lax.ppermute(from_left[..., :half], axis, shift_pairs(count, 1))
    far_b = lax.ppermute(from_right[..., half:], axis, shift_pairs(count, -1))
    far = jnp.concatenate([far_a, far_b], axis=-1)
    relative = jnp.concatenate([block, from_right, far, from_left], axis=along)
    return jnp.roll(relative, me * block.shape[along], axis=along)


def permute_columns(block, order):
    width = block.shape[-1]
    one_hot = (lax.broadcasted_iota(jnp.int32, (width, width), 0) == order[None, :]).astype(block.dtype)
    flat = block.reshape(-1, width)
    moved = jnp.dot(flat, one_hot, preferred_element_type=jnp.float32)
    return moved.astype(block.dtype).reshape(block.shape)


def contract_kernel(s_ref, b_ref, o_ref, out_ref):
    f32 = jnp.float32
    for t in range(s_ref.shape[0]):
        sr = s_ref[t, 0]
        si = s_ref[t, 1]
        br = b_ref[t, 0]
        bi = b_ref[t, 1]
        pr = jnp.dot(sr, br, preferred_element_type=f32) - jnp.dot(si, bi, preferred_element_type=f32)
        pi = jnp.dot(sr, bi, preferred_element_type=f32) + jnp.dot(si, br, preferred_element_type=f32)
        o_r = o_ref[t, 0].astype(f32)
        o_i = o_ref[t, 1].astype(f32)
        re = pr * o_r - pi * o_i
        im = pr * o_i + pi * o_r
        if t == 0:
            out_ref[0] = re
            out_ref[1] = im
        else:
            out_ref[0] += re
            out_ref[1] += im


def contract(stem_t, branch_t, open_t):
    slices, _, rows, width = stem_t.shape
    tile = min(ROW_TILE, rows)
    flops = slices * 8 * rows * width * width
    moved = 2 * (stem_t.size + branch_t.size + open_t.size) + 4 * 2 * rows * width
    return pl.pallas_call(
        contract_kernel,
        out_shape=jax.ShapeDtypeStruct((2, rows, width), jnp.float32),
        grid=(rows // tile,),
        in_specs=[
            pl.BlockSpec((slices, 2, tile, width), lambda i: (0, 0, i, 0)),
            pl.BlockSpec((slices, 2, width, width), lambda i: (0, 0, 0, 0)),
            pl.BlockSpec((slices, 2, tile, width), lambda i: (0, 0, i, 0)),
        ],
        out_specs=pl.BlockSpec((2, tile, width), lambda i: (0, i, 0)),
        cost_estimate=pl.CostEstimate(flops=flops, bytes_accessed=moved, transcendentals=0),
    )(stem_t, branch_t, open_t)


def halving_scatter(blocks, axis):
    count = lax.axis_size(axis)
    me = lax.axis_index(axis)
    shaped = blocks.reshape((2,) + (2,) * 3 + blocks.shape[2:])
    for bit_pos in range(3):
        along = 3 - bit_pos
        bit = (me >> bit_pos) & 1
        keep = lax.dynamic_index_in_dim(shaped, bit, along, keepdims=False)
        send = lax.dynamic_index_in_dim(shaped, 1 - bit, along, keepdims=False)
        pairs = [(i, i ^ (1 << bit_pos)) for i in range(count)]
        shaped = keep + lax.ppermute(send, axis, pairs)
    return shaped


def body(stem_tensor, branch_tensor, open_tensor, open_order):
    slice_count, row_count, _, width = stem_tensor.shape
    permuted = jnp.stack([permute_columns(branch_tensor[t], open_order[t]) for t in range(slice_count)])
    other = lax.ppermute(permuted, "zh", shift_pairs(2, 1))
    low = lax.axis_index("zh") == 0
    pair = jnp.where(low, jnp.stack([permuted, other], axis=1), jnp.stack([other, permuted], axis=1))
    pair = pair[:, :, None, None]
    gathered = ring_gather(pair, "y", 3)
    gathered = ring_gather(gathered, "x", 2)
    gathered = gathered.reshape(slice_count, -1, 2, width)
    branch_t = jnp.transpose(gathered, (0, 2, 1, 3))
    stem_t = jnp.transpose(stem_tensor, (0, 2, 1, 3))
    open_t = jnp.transpose(open_tensor, (0, 2, 1, 3))
    local_sum = contract(stem_t, branch_t, open_t)
    zl_count = lax.axis_size("zl")
    block_rows = row_count // (zl_count * 2)
    shaped = local_sum.reshape(2, zl_count, 2, block_rows, width)
    core = lax.axis_index("core")
    mine = lax.dynamic_index_in_dim(shaped, core, 2, keepdims=False)
    theirs = lax.dynamic_index_in_dim(shaped, 1 - core, 2, keepdims=False)
    mine = mine + lax.ppermute(theirs, "core", shift_pairs(2, 1))
    result = halving_scatter(mine, "zl")
    return jnp.transpose(result, (1, 0, 2)).reshape(1, block_rows, 2, width)


def solution(mesh):
    fine = split_mesh(mesh)
    spec = P(CUTS, STEM, None, None)
    return jax.shard_map(
        body,
        mesh=fine,
        in_specs=(spec, spec, spec, P(CUTS, None)),
        out_specs=P(STEM, CUTS, None, None),
        check_vma=False,
    )
```

```python
import jax
import jax.numpy as jnp
from jax import lax
from jax.experimental import pallas as pl
from jax.sharding import Mesh
from jax.sharding import PartitionSpec as P

CUTS = ("zl", "core")
STEM = ("zh", "x", "y")
ROW_TILE = 256


def split_mesh(mesh):
    devices = mesh.devices.reshape(8, 2, 2, 4, 4)
    return Mesh(devices, CUTS + STEM)


def shift_pairs(count, step):
    return [(i, (i + step) % count) for i in range(count)]


def ring_gather(block, axis):
    count = lax.axis_size(axis)
    from_left = lax.ppermute(block, axis, shift_pairs(count, 1))
    from_right = lax.ppermute(block, axis, shift_pairs(count, -1))
    half = block.shape[-1] // 2
    far_a = lax.ppermute(from_left[..., :half], axis, shift_pairs(count, 1))
    far_b = lax.ppermute(from_right[..., half:], axis, shift_pairs(count, -1))
    far = jnp.concatenate([far_a, far_b], axis=-1)
    return [block, from_right, far, from_left]


def permute_columns(block, order):
    width = block.shape[-1]
    one_hot = (lax.broadcasted_iota(jnp.int32, (width, width), 0) == order[None, :]).astype(block.dtype)
    flat = block.reshape(-1, width)
    moved = jnp.dot(flat, one_hot, preferred_element_type=jnp.float32)
    return moved.astype(block.dtype).reshape(block.shape)


def contract_kernel(s_ref, b_ref, o_ref, out_ref):
    f32 = jnp.float32
    for t in range(s_ref.shape[0]):
        sr = s_ref[t, 0]
        si = s_ref[t, 1]
        br = b_ref[t, 0]
        bi = b_ref[t, 1]
        pr = jnp.dot(sr, br, preferred_element_type=f32) - jnp.dot(si, bi, preferred_element_type=f32)
        pi = jnp.dot(sr, bi, preferred_element_type=f32) + jnp.dot(si, br, preferred_element_type=f32)
        o_r = o_ref[t, 0].astype(f32)
        o_i = o_ref[t, 1].astype(f32)
        re = pr * o_r - pi * o_i
        im = pr * o_i + pi * o_r
        if t == 0:
            out_ref[0] = re
            out_ref[1] = im
        else:
            out_ref[0] += re
            out_ref[1] += im


def contract(stem_t, branch_t, open_t):
    slices, _, rows, width = stem_t.shape
    tile = min(ROW_TILE, rows)
    flops = slices * 8 * rows * width * width
    moved = 2 * (stem_t.size + branch_t.size + open_t.size) + 4 * 2 * rows * width
    return pl.pallas_call(
        contract_kernel,
        out_shape=jax.ShapeDtypeStruct((2, rows, width), jnp.float32),
        grid=(rows // tile,),
        in_specs=[
            pl.BlockSpec((slices, 2, tile, width), lambda i: (0, 0, i, 0)),
            pl.BlockSpec((slices, 2, width, width), lambda i: (0, 0, 0, 0)),
            pl.BlockSpec((slices, 2, tile, width), lambda i: (0, 0, i, 0)),
        ],
        out_specs=pl.BlockSpec((2, tile, width), lambda i: (0, i, 0)),
        cost_estimate=pl.CostEstimate(flops=flops, bytes_accessed=moved, transcendentals=0),
    )(stem_t, branch_t, open_t)


def halving_scatter(blocks, axis):
    count = lax.axis_size(axis)
    me = lax.axis_index(axis)
    shaped = blocks.reshape((2,) + (2,) * 3 + blocks.shape[2:])
    for bit_pos in range(3):
        along = 3 - bit_pos
        bit = (me >> bit_pos) & 1
        keep = lax.dynamic_index_in_dim(shaped, bit, along, keepdims=False)
        send = lax.dynamic_index_in_dim(shaped, 1 - bit, along, keepdims=False)
        pairs = [(i, i ^ (1 << bit_pos)) for i in range(count)]
        shaped = keep + lax.ppermute(send, axis, pairs)
    return shaped


def body(stem_tensor, branch_tensor, open_tensor, open_order):
    slice_count, row_count, _, width = stem_tensor.shape
    permuted = jnp.stack([permute_columns(branch_tensor[t], open_order[t]) for t in range(slice_count)])
    permuted = jnp.transpose(permuted, (0, 2, 1, 3))
    other = lax.ppermute(permuted, "zh", shift_pairs(2, 1))
    low = lax.axis_index("zh") == 0
    pair = jnp.where(low, jnp.stack([permuted, other], axis=2), jnp.stack([other, permuted], axis=2))
    y_block = jnp.stack(ring_gather(pair, "y"), axis=3)
    x_pieces = ring_gather(y_block, "x")
    branch_t = jnp.concatenate(
        [piece.reshape(slice_count, 2, -1, width) for piece in x_pieces], axis=2
    )
    x = lax.axis_index("x")
    y = lax.axis_index("y")
    x_count = lax.axis_size("x")
    y_count = lax.axis_size("y")
    stem6 = stem_tensor.reshape(slice_count, row_count, 2, 2, x_count, y_count, -1)
    stem6 = jnp.roll(stem6, -x, axis=4)
    stem6 = jnp.roll(stem6, -y, axis=5)
    stem_t = jnp.transpose(stem6, (0, 2, 1, 4, 3, 5, 6)).reshape(slice_count, 2, row_count, width)
    open_t = jnp.transpose(open_tensor, (0, 2, 1, 3))
    local_sum = contract(stem_t, branch_t, open_t)
    zl_count = lax.axis_size("zl")
    block_rows = row_count // (zl_count * 2)
    shaped = local_sum.reshape(2, zl_count, 2, block_rows, width)
    core = lax.axis_index("core")
    mine = lax.dynamic_index_in_dim(shaped, core, 2, keepdims=False)
    theirs = lax.dynamic_index_in_dim(shaped, 1 - core, 2, keepdims=False)
    mine = mine + lax.ppermute(theirs, "core", shift_pairs(2, 1))
    result = halving_scatter(mine, "zl")
    return jnp.transpose(result, (1, 0, 2)).reshape(1, block_rows, 2, width)


def solution(mesh):
    fine = split_mesh(mesh)
    spec = P(CUTS, STEM, None, None)
    return jax.shard_map(
        body,
        mesh=fine,
        in_specs=(spec, spec, spec, P(CUTS, None)),
        out_specs=P(STEM, CUTS, None, None),
        check_vma=False,
    )
```

```python
import jax
import jax.numpy as jnp
from jax import lax
from jax.experimental import pallas as pl
from jax.sharding import Mesh
from jax.sharding import PartitionSpec as P

CUTS = ("zl", "core")
STEM = ("zh", "x", "y")
ROW_TILE = 256


def split_mesh(mesh):
    devices = mesh.devices.reshape(8, 2, 2, 4, 4)
    return Mesh(devices, CUTS + STEM)


def shift_pairs(count, step):
    return [(i, (i + step) % count) for i in range(count)]


def ring_gather(block, axis):
    count = lax.axis_size(axis)
    from_left = lax.ppermute(block, axis, shift_pairs(count, 1))
    from_right = lax.ppermute(block, axis, shift_pairs(count, -1))
    half = block.shape[-1] // 2
    far_a = lax.ppermute(from_left[..., :half], axis, shift_pairs(count, 1))
    far_b = lax.ppermute(from_right[..., half:], axis, shift_pairs(count, -1))
    far = jnp.concatenate([far_a, far_b], axis=-1)
    return [block, from_right, far, from_left]


def permute_columns(block, order):
    width = block.shape[-1]
    one_hot = (lax.broadcasted_iota(jnp.int32, (width, width), 0) == order[None, :]).astype(block.dtype)
    flat = block.reshape(-1, width)
    moved = jnp.dot(flat, one_hot, preferred_element_type=jnp.float32)
    return moved.astype(block.dtype).reshape(block.shape)


def contract_kernel(s_ref, b_ref, o_ref, out_ref):
    f32 = jnp.float32
    for t in range(s_ref.shape[0]):
        sr = s_ref[t, 0]
        si = s_ref[t, 1]
        br = b_ref[t, 0]
        bi = b_ref[t, 1]
        pr = jnp.dot(sr, br, preferred_element_type=f32) - jnp.dot(si, bi, preferred_element_type=f32)
        pi = jnp.dot(sr, bi, preferred_element_type=f32) + jnp.dot(si, br, preferred_element_type=f32)
        o_r = o_ref[t, 0].astype(f32)
        o_i = o_ref[t, 1].astype(f32)
        re = pr * o_r - pi * o_i
        im = pr * o_i + pi * o_r
        if t == 0:
            out_ref[0] = re
            out_ref[1] = im
        else:
            out_ref[0] += re
            out_ref[1] += im


def contract(stem_t, branch_t, open_t):
    slices, _, rows, width = stem_t.shape
    tile = min(ROW_TILE, rows)
    flops = slices * 8 * rows * width * width
    moved = 2 * (stem_t.size + branch_t.size + open_t.size) + 4 * 2 * rows * width
    return pl.pallas_call(
        contract_kernel,
        out_shape=jax.ShapeDtypeStruct((2, rows, width), jnp.float32),
        grid=(rows // tile,),
        in_specs=[
            pl.BlockSpec((slices, 2, tile, width), lambda i: (0, 0, i, 0)),
            pl.BlockSpec((slices, 2, width, width), lambda i: (0, 0, 0, 0)),
            pl.BlockSpec((slices, 2, tile, width), lambda i: (0, 0, i, 0)),
        ],
        out_specs=pl.BlockSpec((2, tile, width), lambda i: (0, i, 0)),
        cost_estimate=pl.CostEstimate(flops=flops, bytes_accessed=moved, transcendentals=0),
    )(stem_t, branch_t, open_t)


def halving_scatter(blocks, axis):
    count = lax.axis_size(axis)
    me = lax.axis_index(axis)
    shaped = blocks.reshape((2,) + (2,) * 3 + blocks.shape[2:])
    for bit_pos in range(3):
        along = 3 - bit_pos
        bit = (me >> bit_pos) & 1
        keep = lax.dynamic_index_in_dim(shaped, bit, along, keepdims=False)
        send = lax.dynamic_index_in_dim(shaped, 1 - bit, along, keepdims=False)
        pairs = [(i, i ^ (1 << bit_pos)) for i in range(count)]
        shaped = keep + lax.ppermute(send, axis, pairs)
    return shaped


def body(stem_tensor, branch_tensor, open_tensor, open_order):
    slice_count, row_count, _, width = stem_tensor.shape
    permuted = jnp.stack([permute_columns(branch_tensor[t], open_order[t]) for t in range(slice_count)])
    permuted = jnp.transpose(permuted, (0, 2, 1, 3))
    other = lax.ppermute(permuted, "zh", shift_pairs(2, 1))
    low = lax.axis_index("zh") == 0
    pair = jnp.where(low, jnp.stack([permuted, other], axis=2), jnp.stack([other, permuted], axis=2))
    plane = lax.axis_size("x") * lax.axis_size("y")
    copies = jnp.broadcast_to(pair[:, :, None], pair.shape[:2] + (plane,) + pair.shape[2:])
    copies = copies.reshape(slice_count, 2, plane, -1, width)
    gathered = lax.all_to_all(copies, ("x", "y"), 2, 2, tiled=True)
    branch_t = gathered.reshape(slice_count, 2, -1, width)
    x_count = lax.axis_size("x")
    y_count = lax.axis_size("y")
    stem6 = stem_tensor.reshape(slice_count, row_count, 2, 2, x_count, y_count, -1)
    stem_t = jnp.transpose(stem6, (0, 2, 1, 4, 5, 3, 6)).reshape(slice_count, 2, row_count, width)
    open_t = jnp.transpose(open_tensor, (0, 2, 1, 3))
    local_sum = contract(stem_t, branch_t, open_t)
    zl_count = lax.axis_size("zl")
    block_rows = row_count // (zl_count * 2)
    shaped = local_sum.reshape(2, zl_count, 2, block_rows, width)
    core = lax.axis_index("core")
    mine = lax.dynamic_index_in_dim(shaped, core, 2, keepdims=False)
    theirs = lax.dynamic_index_in_dim(shaped, 1 - core, 2, keepdims=False)
    mine = mine + lax.ppermute(theirs, "core", shift_pairs(2, 1))
    result = halving_scatter(mine, "zl")
    return jnp.transpose(result, (1, 0, 2)).reshape(1, block_rows, 2, width)


def solution(mesh):
    fine = split_mesh(mesh)
    spec = P(CUTS, STEM, None, None)
    return jax.shard_map(
        body,
        mesh=fine,
        in_specs=(spec, spec, spec, P(CUTS, None)),
        out_specs=P(STEM, CUTS, None, None),
        check_vma=False,
    )
```

```python
import jax
import jax.numpy as jnp
from jax import lax
from jax.experimental import pallas as pl
from jax.sharding import Mesh
from jax.sharding import PartitionSpec as P

CUTS = ("zl", "core")
STEM = ("zh", "x", "y")
ROW_TILE = 256


def split_mesh(mesh):
    devices = mesh.devices.reshape(8, 2, 2, 4, 4)
    return Mesh(devices, CUTS + STEM)


def shift_pairs(count, step):
    return [(i, (i + step) % count) for i in range(count)]


def ring_gather(block, axis):
    count = lax.axis_size(axis)
    from_left = lax.ppermute(block, axis, shift_pairs(count, 1))
    from_right = lax.ppermute(block, axis, shift_pairs(count, -1))
    half = block.shape[-1] // 2
    far_a = lax.ppermute(from_left[..., :half], axis, shift_pairs(count, 1))
    far_b = lax.ppermute(from_right[..., half:], axis, shift_pairs(count, -1))
    far = jnp.concatenate([far_a, far_b], axis=-1)
    return [block, from_right, far, from_left]


def permute_columns(block, order):
    width = block.shape[-1]
    one_hot = (lax.broadcasted_iota(jnp.int32, (width, width), 0) == order[None, :]).astype(block.dtype)
    flat = block.reshape(-1, width)
    moved = jnp.dot(flat, one_hot, preferred_element_type=jnp.float32)
    return moved.astype(block.dtype).reshape(block.shape)


def contract_kernel(s_ref, b_ref, o_ref, out_ref):
    f32 = jnp.float32
    for t in range(s_ref.shape[0]):
        sr = s_ref[t, :, 0, :]
        si = s_ref[t, :, 1, :]
        br = b_ref[t, 0]
        bi = b_ref[t, 1]
        pr = jnp.dot(sr, br, preferred_element_type=f32) - jnp.dot(si, bi, preferred_element_type=f32)
        pi = jnp.dot(sr, bi, preferred_element_type=f32) + jnp.dot(si, br, preferred_element_type=f32)
        o_r = o_ref[t, :, 0, :].astype(f32)
        o_i = o_ref[t, :, 1, :].astype(f32)
        re = pr * o_r - pi * o_i
        im = pr * o_i + pi * o_r
        if t == 0:
            out_ref[0] = re
            out_ref[1] = im
        else:
            out_ref[0] += re
            out_ref[1] += im


def contract(stem_t, branch_t, open_t):
    slices, rows, _, width = stem_t.shape
    tile = min(ROW_TILE, rows)
    flops = slices * 8 * rows * width * width
    moved = 2 * (stem_t.size + branch_t.size + open_t.size) + 4 * 2 * rows * width
    return pl.pallas_call(
        contract_kernel,
        out_shape=jax.ShapeDtypeStruct((2, rows, width), jnp.float32),
        grid=(rows // tile,),
        in_specs=[
            pl.BlockSpec((slices, tile, 2, width), lambda i: (0, i, 0, 0)),
            pl.BlockSpec((slices, 2, width, width), lambda i: (0, 0, 0, 0)),
            pl.BlockSpec((slices, tile, 2, width), lambda i: (0, i, 0, 0)),
        ],
        out_specs=pl.BlockSpec((2, tile, width), lambda i: (0, i, 0)),
        cost_estimate=pl.CostEstimate(flops=flops, bytes_accessed=moved, transcendentals=0),
    )(stem_t, branch_t, open_t)


def halving_scatter(blocks, axis):
    count = lax.axis_size(axis)
    me = lax.axis_index(axis)
    shaped = blocks.reshape((2,) + (2,) * 3 + blocks.shape[2:])
    for bit_pos in range(3):
        along = 3 - bit_pos
        bit = (me >> bit_pos) & 1
        keep = lax.dynamic_index_in_dim(shaped, bit, along, keepdims=False)
        send = lax.dynamic_index_in_dim(shaped, 1 - bit, along, keepdims=False)
        pairs = [(i, i ^ (1 << bit_pos)) for i in range(count)]
        shaped = keep + lax.ppermute(send, axis, pairs)
    return shaped


def body(stem_tensor, branch_tensor, open_tensor, open_order):
    slice_count, row_count, _, width = stem_tensor.shape
    permuted = jnp.stack([permute_columns(branch_tensor[t], open_order[t]) for t in range(slice_count)])
    permuted = jnp.transpose(permuted, (0, 2, 1, 3))
    other = lax.ppermute(permuted, "zh", shift_pairs(2, 1))
    low = lax.axis_index("zh") == 0
    pair = jnp.where(low, jnp.stack([permuted, other], axis=2), jnp.stack([other, permuted], axis=2))
    plane = lax.axis_size("x") * lax.axis_size("y")
    copies = jnp.broadcast_to(pair[:, :, None], pair.shape[:2] + (plane,) + pair.shape[2:])
    gathered = lax.all_to_all(copies, ("x", "y"), 2, 4, tiled=True)
    branch_t = gathered.reshape(slice_count, 2, -1, width)
    stem_t = stem_tensor
    open_t = open_tensor
    local_sum = contract(stem_t, branch_t, open_t)
    zl_count = lax.axis_size("zl")
    block_rows = row_count // (zl_count * 2)
    shaped = local_sum.reshape(2, zl_count, 2, block_rows, width)
    core = lax.axis_index("core")
    mine = lax.dynamic_index_in_dim(shaped, core, 2, keepdims=False)
    theirs = lax.dynamic_index_in_dim(shaped, 1 - core, 2, keepdims=False)
    mine = mine + lax.ppermute(theirs, "core", shift_pairs(2, 1))
    result = halving_scatter(mine, "zl")
    return jnp.transpose(result, (1, 0, 2)).reshape(1, block_rows, 2, width)


def solution(mesh):
    fine = split_mesh(mesh)
    spec = P(CUTS, STEM, None, None)
    return jax.shard_map(
        body,
        mesh=fine,
        in_specs=(spec, spec, spec, P(CUTS, None)),
        out_specs=P(STEM, CUTS, None, None),
        check_vma=False,
    )
```

```python
import jax
import jax.numpy as jnp
from jax import lax
from jax.experimental import pallas as pl
from jax.sharding import Mesh
from jax.sharding import PartitionSpec as P

CUTS = ("zl", "core")
STEM = ("zh", "x", "y")
ROW_TILE = 256


def split_mesh(mesh):
    devices = mesh.devices.reshape(8, 2, 2, 4, 4)
    return Mesh(devices, CUTS + STEM)


def shift_pairs(count, step):
    return [(i, (i + step) % count) for i in range(count)]


def ring_gather(block, axis):
    count = lax.axis_size(axis)
    from_left = lax.ppermute(block, axis, shift_pairs(count, 1))
    from_right = lax.ppermute(block, axis, shift_pairs(count, -1))
    half = block.shape[-1] // 2
    far_a = lax.ppermute(from_left[..., :half], axis, shift_pairs(count, 1))
    far_b = lax.ppermute(from_right[..., half:], axis, shift_pairs(count, -1))
    far = jnp.concatenate([far_a, far_b], axis=-1)
    return [block, from_right, far, from_left]


def permute_columns(block, order):
    width = block.shape[-1]
    one_hot = (lax.broadcasted_iota(jnp.int32, (width, width), 0) == order[None, :]).astype(block.dtype)
    flat = block.reshape(-1, width)
    moved = jnp.dot(flat, one_hot, preferred_element_type=jnp.float32)
    return moved.astype(block.dtype).reshape(block.shape)


def contract_kernel(s_ref, b_ref, o_ref, out_ref):
    f32 = jnp.float32
    for t in range(s_ref.shape[0]):
        sr = s_ref[t, 0]
        si = s_ref[t, 1]
        br = b_ref[t, 0]
        bi = b_ref[t, 1]
        pr = jnp.dot(sr, br, preferred_element_type=f32) - jnp.dot(si, bi, preferred_element_type=f32)
        pi = jnp.dot(sr, bi, preferred_element_type=f32) + jnp.dot(si, br, preferred_element_type=f32)
        o_r = o_ref[t, 0].astype(f32)
        o_i = o_ref[t, 1].astype(f32)
        re = pr * o_r - pi * o_i
        im = pr * o_i + pi * o_r
        if t == 0:
            out_ref[0] = re
            out_ref[1] = im
        else:
            out_ref[0] += re
            out_ref[1] += im


def contract(stem_t, branch_t, open_t, column_block):
    slices, _, rows, depth = stem_t.shape
    width = branch_t.shape[-1]
    tile = min(ROW_TILE, rows)
    flops = slices * 8 * rows * depth * width
    moved = 2 * (stem_t.size + branch_t.size) + 2 * slices * 2 * rows * width + 4 * 2 * rows * width
    return pl.pallas_call(
        contract_kernel,
        out_shape=jax.ShapeDtypeStruct((2, rows, width), jnp.float32),
        grid=(rows // tile,),
        in_specs=[
            pl.BlockSpec((slices, 2, tile, depth), lambda i: (0, 0, i, 0)),
            pl.BlockSpec((slices, 2, depth, width), lambda i: (0, 0, 0, 0)),
            pl.BlockSpec((slices, 2, tile, width), lambda i: (0, 0, i, column_block)),
        ],
        out_specs=pl.BlockSpec((2, tile, width), lambda i: (0, i, 0)),
        cost_estimate=pl.CostEstimate(flops=flops, bytes_accessed=moved, transcendentals=0),
    )(stem_t, branch_t, open_t)


def halving_scatter(blocks, axis):
    count = lax.axis_size(axis)
    me = lax.axis_index(axis)
    shaped = blocks.reshape((2,) + (2,) * 3 + blocks.shape[2:])
    for bit_pos in range(3):
        along = 3 - bit_pos
        bit = (me >> bit_pos) & 1
        keep = lax.dynamic_index_in_dim(shaped, bit, along, keepdims=False)
        send = lax.dynamic_index_in_dim(shaped, 1 - bit, along, keepdims=False)
        pairs = [(i, i ^ (1 << bit_pos)) for i in range(count)]
        shaped = keep + lax.ppermute(send, axis, pairs)
    return shaped


def body(stem_tensor, branch_tensor, open_tensor, open_order):
    slice_count, row_count, _, width = stem_tensor.shape
    permuted = jnp.stack([permute_columns(branch_tensor[t], open_order[t]) for t in range(slice_count)])
    permuted = jnp.transpose(permuted, (0, 2, 1, 3))
    other = lax.ppermute(permuted, "zh", shift_pairs(2, 1))
    low = lax.axis_index("zh") == 0
    pair = jnp.where(low, jnp.stack([permuted, other], axis=2), jnp.stack([other, permuted], axis=2))
    plane = lax.axis_size("x") * lax.axis_size("y")
    copies = jnp.broadcast_to(pair[:, :, None], pair.shape[:2] + (plane,) + pair.shape[2:])
    copies = copies.reshape(slice_count, 2, plane, -1, width)
    halves = 2
    span = width // halves
    x_count = lax.axis_size("x")
    y_count = lax.axis_size("y")
    stem6 = stem_tensor.reshape(slice_count, row_count, 2, 2, x_count, y_count, -1)
    stem_t = jnp.transpose(stem6, (0, 2, 1, 4, 5, 3, 6)).reshape(slice_count, 2, row_count, width)
    open_t = jnp.transpose(open_tensor, (0, 2, 1, 3))
    zl_count = lax.axis_size("zl")
    block_rows = row_count // (zl_count * 2)
    core = lax.axis_index("core")
    results = []
    previous = None
    for h in range(halves):
        part = copies[..., h * span:(h + 1) * span]
        if previous is not None:
            part, previous = lax.optimization_barrier((part, previous))
        gathered = lax.all_to_all(part, ("x", "y"), 2, 2, tiled=True)
        previous = gathered
        branch_t = gathered.reshape(slice_count, 2, -1, span)
        local_sum = contract(stem_t, branch_t, open_t, h)
        shaped = local_sum.reshape(2, zl_count, 2, block_rows, span)
        mine = lax.dynamic_index_in_dim(shaped, core, 2, keepdims=False)
        theirs = lax.dynamic_index_in_dim(shaped, 1 - core, 2, keepdims=False)
        mine = mine + lax.ppermute(theirs, "core", shift_pairs(2, 1))
        results.append(halving_scatter(mine, "zl"))
    result = jnp.concatenate(results, axis=-1)
    return jnp.transpose(result, (1, 0, 2)).reshape(1, block_rows, 2, width)


def solution(mesh):
    fine = split_mesh(mesh)
    spec = P(CUTS, STEM, None, None)
    return jax.shard_map(
        body,
        mesh=fine,
        in_specs=(spec, spec, spec, P(CUTS, None)),
        out_specs=P(STEM, CUTS, None, None),
        check_vma=False,
    )
```

```python
import jax
import jax.numpy as jnp
from jax import lax
from jax.experimental import pallas as pl
from jax.sharding import Mesh
from jax.sharding import PartitionSpec as P

CUTS = ("zl", "core")
STEM = ("zh", "x", "y")
ROW_TILE = 256


def split_mesh(mesh):
    devices = mesh.devices.reshape(8, 2, 2, 4, 4)
    return Mesh(devices, CUTS + STEM)


def shift_pairs(count, step):
    return [(i, (i + step) % count) for i in range(count)]


def ring_gather(block, axis):
    count = lax.axis_size(axis)
    from_left = lax.ppermute(block, axis, shift_pairs(count, 1))
    from_right = lax.ppermute(block, axis, shift_pairs(count, -1))
    half = block.shape[-1] // 2
    far_a = lax.ppermute(from_left[..., :half], axis, shift_pairs(count, 1))
    far_b = lax.ppermute(from_right[..., half:], axis, shift_pairs(count, -1))
    far = jnp.concatenate([far_a, far_b], axis=-1)
    return [block, from_right, far, from_left]


def permute_columns(block, order):
    width = block.shape[-1]
    one_hot = (lax.broadcasted_iota(jnp.int32, (width, width), 0) == order[None, :]).astype(block.dtype)
    flat = block.reshape(-1, width)
    moved = jnp.dot(flat, one_hot, preferred_element_type=jnp.float32)
    return moved.astype(block.dtype).reshape(block.shape)


def contract_kernel(s_ref, b_ref, o_ref, out_ref):
    f32 = jnp.float32
    for t in range(s_ref.shape[0]):
        sr = s_ref[t, :, 0, :]
        si = s_ref[t, :, 1, :]
        br = b_ref[t, 0]
        bi = b_ref[t, 1]
        pr = jnp.dot(sr, br, preferred_element_type=f32) - jnp.dot(si, bi, preferred_element_type=f32)
        pi = jnp.dot(sr, bi, preferred_element_type=f32) + jnp.dot(si, br, preferred_element_type=f32)
        o_r = o_ref[t, :, 0, :].astype(f32)
        o_i = o_ref[t, :, 1, :].astype(f32)
        re = pr * o_r - pi * o_i
        im = pr * o_i + pi * o_r
        if t == 0:
            out_ref[0] = re
            out_ref[1] = im
        else:
            out_ref[0] += re
            out_ref[1] += im


def contract(stem_t, branch_t, open_t, column_block):
    slices, rows, _, depth = stem_t.shape
    width = branch_t.shape[-1]
    tile = min(ROW_TILE, rows)
    flops = slices * 8 * rows * depth * width
    moved = 2 * (stem_t.size + branch_t.size) + 2 * slices * 2 * rows * width + 4 * 2 * rows * width
    return pl.pallas_call(
        contract_kernel,
        out_shape=jax.ShapeDtypeStruct((2, rows, width), jnp.float32),
        grid=(rows // tile,),
        in_specs=[
            pl.BlockSpec((slices, tile, 2, depth), lambda i: (0, i, 0, 0)),
            pl.BlockSpec((slices, 2, depth, width), lambda i: (0, 0, 0, 0)),
            pl.BlockSpec((slices, tile, 2, width), lambda i: (0, i, 0, column_block)),
        ],
        out_specs=pl.BlockSpec((2, tile, width), lambda i: (0, i, 0)),
        cost_estimate=pl.CostEstimate(flops=flops, bytes_accessed=moved, transcendentals=0),
    )(stem_t, branch_t, open_t)


def halving_scatter(blocks, axis):
    count = lax.axis_size(axis)
    me = lax.axis_index(axis)
    shaped = blocks.reshape((2,) + (2,) * 3 + blocks.shape[2:])
    for bit_pos in range(3):
        along = 3 - bit_pos
        bit = (me >> bit_pos) & 1
        keep = lax.dynamic_index_in_dim(shaped, bit, along, keepdims=False)
        send = lax.dynamic_index_in_dim(shaped, 1 - bit, along, keepdims=False)
        pairs = [(i, i ^ (1 << bit_pos)) for i in range(count)]
        shaped = keep + lax.ppermute(send, axis, pairs)
    return shaped


def body(stem_tensor, branch_tensor, open_tensor, open_order):
    slice_count, row_count, _, width = stem_tensor.shape
    permuted = jnp.stack([permute_columns(branch_tensor[t], open_order[t]) for t in range(slice_count)])
    permuted = jnp.transpose(permuted, (0, 2, 1, 3))
    other = lax.ppermute(permuted, "zh", shift_pairs(2, 1))
    low = lax.axis_index("zh") == 0
    pair = jnp.where(low, jnp.stack([permuted, other], axis=2), jnp.stack([other, permuted], axis=2))
    plane = lax.axis_size("x") * lax.axis_size("y")
    copies = jnp.broadcast_to(pair[:, :, None], pair.shape[:2] + (plane,) + pair.shape[2:])
    halves = 2
    span = width // halves
    stem_t = stem_tensor
    open_t = open_tensor
    zl_count = lax.axis_size("zl")
    block_rows = row_count // (zl_count * 2)
    core = lax.axis_index("core")
    results = []
    previous = None
    for h in range(halves):
        part = copies[..., h * span:(h + 1) * span]
        if previous is not None:
            part, previous = lax.optimization_barrier((part, previous))
        gathered = lax.all_to_all(part, ("x", "y"), 2, 4, tiled=True)
        previous = gathered
        branch_t = gathered.reshape(slice_count, 2, -1, span)
        local_sum = contract(stem_t, branch_t, open_t, h)
        shaped = local_sum.reshape(2, zl_count, 2, block_rows, span)
        mine = lax.dynamic_index_in_dim(shaped, core, 2, keepdims=False)
        theirs = lax.dynamic_index_in_dim(shaped, 1 - core, 2, keepdims=False)
        mine = mine + lax.ppermute(theirs, "core", shift_pairs(2, 1))
        results.append(halving_scatter(mine, "zl"))
    result = jnp.concatenate(results, axis=-1)
    return jnp.transpose(result, (1, 0, 2)).reshape(1, block_rows, 2, width)


def solution(mesh):
    fine = split_mesh(mesh)
    spec = P(CUTS, STEM, None, None)
    return jax.shard_map(
        body,
        mesh=fine,
        in_specs=(spec, spec, spec, P(CUTS, None)),
        out_specs=P(STEM, CUTS, None, None),
        check_vma=False,
    )
```

```python
import jax
import jax.numpy as jnp
from jax import lax
from jax.experimental import pallas as pl
from jax.sharding import Mesh
from jax.sharding import PartitionSpec as P

CUTS = ("zl", "core")
STEM = ("zh", "x", "y")
ROW_TILE = 256


def split_mesh(mesh):
    devices = mesh.devices.reshape(8, 2, 2, 4, 4)
    return Mesh(devices, CUTS + STEM)


def shift_pairs(count, step):
    return [(i, (i + step) % count) for i in range(count)]


def ring_gather(block, axis):
    count = lax.axis_size(axis)
    from_left = lax.ppermute(block, axis, shift_pairs(count, 1))
    from_right = lax.ppermute(block, axis, shift_pairs(count, -1))
    half = block.shape[-1] // 2
    far_a = lax.ppermute(from_left[..., :half], axis, shift_pairs(count, 1))
    far_b = lax.ppermute(from_right[..., half:], axis, shift_pairs(count, -1))
    far = jnp.concatenate([far_a, far_b], axis=-1)
    return [block, from_right, far, from_left]


def permute_columns(block, order):
    width = block.shape[-1]
    one_hot = (lax.broadcasted_iota(jnp.int32, (width, width), 0) == order[None, :]).astype(block.dtype)
    flat = block.reshape(-1, width)
    moved = jnp.dot(flat, one_hot, preferred_element_type=jnp.float32)
    return moved.astype(block.dtype).reshape(block.shape)


def contract_kernel(s_ref, b_ref, o_ref, out_ref):
    f32 = jnp.float32
    for t in range(s_ref.shape[0]):
        sr = s_ref[t, 0]
        si = s_ref[t, 1]
        br = b_ref[t, 0]
        bi = b_ref[t, 1]
        pr = jnp.dot(sr, br, preferred_element_type=f32) - jnp.dot(si, bi, preferred_element_type=f32)
        pi = jnp.dot(sr, bi, preferred_element_type=f32) + jnp.dot(si, br, preferred_element_type=f32)
        o_r = o_ref[t, :, 0, :].astype(f32)
        o_i = o_ref[t, :, 1, :].astype(f32)
        re = pr * o_r - pi * o_i
        im = pr * o_i + pi * o_r
        if t == 0:
            out_ref[0] = re
            out_ref[1] = im
        else:
            out_ref[0] += re
            out_ref[1] += im


def contract(stem_t, branch_t, open_t, column_block):
    slices, _, rows, depth = stem_t.shape
    width = branch_t.shape[-1]
    tile = min(ROW_TILE, rows)
    flops = slices * 8 * rows * depth * width
    moved = 2 * (stem_t.size + branch_t.size) + 2 * slices * 2 * rows * width + 4 * 2 * rows * width
    return pl.pallas_call(
        contract_kernel,
        out_shape=jax.ShapeDtypeStruct((2, rows, width), jnp.float32),
        grid=(rows // tile,),
        in_specs=[
            pl.BlockSpec((slices, 2, tile, depth), lambda i: (0, 0, i, 0)),
            pl.BlockSpec((slices, 2, depth, width), lambda i: (0, 0, 0, 0)),
            pl.BlockSpec((slices, tile, 2, width), lambda i: (0, i, 0, column_block)),
        ],
        out_specs=pl.BlockSpec((2, tile, width), lambda i: (0, i, 0)),
        cost_estimate=pl.CostEstimate(flops=flops, bytes_accessed=moved, transcendentals=0),
    )(stem_t, branch_t, open_t)


def halving_scatter(blocks, axis):
    count = lax.axis_size(axis)
    me = lax.axis_index(axis)
    shaped = blocks.reshape((2,) + (2,) * 3 + blocks.shape[2:])
    for bit_pos in range(3):
        along = 3 - bit_pos
        bit = (me >> bit_pos) & 1
        keep = lax.dynamic_index_in_dim(shaped, bit, along, keepdims=False)
        send = lax.dynamic_index_in_dim(shaped, 1 - bit, along, keepdims=False)
        pairs = [(i, i ^ (1 << bit_pos)) for i in range(count)]
        shaped = keep + lax.ppermute(send, axis, pairs)
    return shaped


def body(stem_tensor, branch_tensor, open_tensor, open_order):
    slice_count, row_count, _, width = stem_tensor.shape
    permuted = jnp.stack([permute_columns(branch_tensor[t], open_order[t]) for t in range(slice_count)])
    permuted = jnp.transpose(permuted, (0, 2, 1, 3))
    other = lax.ppermute(permuted, "zh", shift_pairs(2, 1))
    low = lax.axis_index("zh") == 0
    pair = jnp.where(low, jnp.stack([permuted, other], axis=2), jnp.stack([other, permuted], axis=2))
    plane = lax.axis_size("x") * lax.axis_size("y")
    copies = jnp.broadcast_to(pair[:, :, None], pair.shape[:2] + (plane,) + pair.shape[2:])
    halves = 2
    span = width // halves
    stem_t = jnp.transpose(stem_tensor, (0, 2, 1, 3))
    open_t = open_tensor
    zl_count = lax.axis_size("zl")
    block_rows = row_count // (zl_count * 2)
    core = lax.axis_index("core")
    results = []
    previous = None
    for h in range(halves):
        part = copies[..., h * span:(h + 1) * span]
        if previous is not None:
            part, previous = lax.optimization_barrier((part, previous))
        gathered = lax.all_to_all(part, ("x", "y"), 2, 4, tiled=True)
        previous = gathered
        branch_t = gathered.reshape(slice_count, 2, -1, span)
        local_sum = contract(stem_t, branch_t, open_t, h)
        shaped = local_sum.reshape(2, zl_count, 2, block_rows, span)
        mine = lax.dynamic_index_in_dim(shaped, core, 2, keepdims=False)
        theirs = lax.dynamic_index_in_dim(shaped, 1 - core, 2, keepdims=False)
        mine = mine + lax.ppermute(theirs, "core", shift_pairs(2, 1))
        results.append(halving_scatter(mine, "zl"))
    result = jnp.concatenate(results, axis=-1)
    return jnp.transpose(result, (1, 0, 2)).reshape(1, block_rows, 2, width)


def solution(mesh):
    fine = split_mesh(mesh)
    spec = P(CUTS, STEM, None, None)
    return jax.shard_map(
        body,
        mesh=fine,
        in_specs=(spec, spec, spec, P(CUTS, None)),
        out_specs=P(STEM, CUTS, None, None),
        check_vma=False,
    )
```

```python
import jax
import jax.numpy as jnp
from jax import lax
from jax.experimental import pallas as pl
from jax.sharding import Mesh
from jax.sharding import PartitionSpec as P

CUTS = ("zq", "zb", "core")
STEM = ("zh", "x", "y")
ROW_TILE = 256


def split_mesh(mesh):
    devices = mesh.devices.reshape(4, 2, 2, 2, 4, 4)
    return Mesh(devices, CUTS + STEM)


def shift_pairs(count, step):
    return [(i, (i + step) % count) for i in range(count)]


def ring_gather(block, axis):
    count = lax.axis_size(axis)
    from_left = lax.ppermute(block, axis, shift_pairs(count, 1))
    from_right = lax.ppermute(block, axis, shift_pairs(count, -1))
    half = block.shape[-1] // 2
    far_a = lax.ppermute(from_left[..., :half], axis, shift_pairs(count, 1))
    far_b = lax.ppermute(from_right[..., half:], axis, shift_pairs(count, -1))
    far = jnp.concatenate([far_a, far_b], axis=-1)
    return [block, from_right, far, from_left]


def permute_columns(block, order):
    width = block.shape[-1]
    one_hot = (lax.broadcasted_iota(jnp.int32, (width, width), 0) == order[None, :]).astype(block.dtype)
    flat = block.reshape(-1, width)
    moved = jnp.dot(flat, one_hot, preferred_element_type=jnp.float32)
    return moved.astype(block.dtype).reshape(block.shape)


def contract_kernel(s_ref, b_ref, o_ref, out_ref):
    f32 = jnp.float32
    for t in range(s_ref.shape[0]):
        sr = s_ref[t, 0]
        si = s_ref[t, 1]
        br = b_ref[t, 0]
        bi = b_ref[t, 1]
        pr = jnp.dot(sr, br, preferred_element_type=f32) - jnp.dot(si, bi, preferred_element_type=f32)
        pi = jnp.dot(sr, bi, preferred_element_type=f32) + jnp.dot(si, br, preferred_element_type=f32)
        o_r = o_ref[t, :, 0, :].astype(f32)
        o_i = o_ref[t, :, 1, :].astype(f32)
        re = pr * o_r - pi * o_i
        im = pr * o_i + pi * o_r
        if t == 0:
            out_ref[0] = re
            out_ref[1] = im
        else:
            out_ref[0] += re
            out_ref[1] += im


def contract(stem_t, branch_t, open_t, column_block):
    slices, _, rows, depth = stem_t.shape
    width = branch_t.shape[-1]
    tile = min(ROW_TILE, rows)
    flops = slices * 8 * rows * depth * width
    moved = 2 * (stem_t.size + branch_t.size) + 2 * slices * 2 * rows * width + 4 * 2 * rows * width
    return pl.pallas_call(
        contract_kernel,
        out_shape=jax.ShapeDtypeStruct((2, rows, width), jnp.float32),
        grid=(rows // tile,),
        in_specs=[
            pl.BlockSpec((slices, 2, tile, depth), lambda i: (0, 0, i, 0)),
            pl.BlockSpec((slices, 2, depth, width), lambda i: (0, 0, 0, 0)),
            pl.BlockSpec((slices, tile, 2, width), lambda i: (0, i, 0, column_block)),
        ],
        out_specs=pl.BlockSpec((2, tile, width), lambda i: (0, i, 0)),
        cost_estimate=pl.CostEstimate(flops=flops, bytes_accessed=moved, transcendentals=0),
    )(stem_t, branch_t, open_t)


def cuts_scatter(blocks):
    zb = lax.axis_index("zb")
    shaped = blocks.reshape((2, lax.axis_size("zq"), 2) + blocks.shape[2:])
    keep = lax.dynamic_index_in_dim(shaped, zb, 2, keepdims=False)
    send = lax.dynamic_index_in_dim(shaped, 1 - zb, 2, keepdims=False)
    part = keep + lax.ppermute(send, "zb", shift_pairs(2, 1))
    got = lax.all_to_all(part, "zq", 1, 1, tiled=True)
    return jnp.sum(got, axis=1)


def body(stem_tensor, branch_tensor, open_tensor, open_order):
    slice_count, row_count, _, width = stem_tensor.shape
    permuted = jnp.stack([permute_columns(branch_tensor[t], open_order[t]) for t in range(slice_count)])
    permuted = jnp.transpose(permuted, (0, 2, 1, 3))
    other = lax.ppermute(permuted, "zh", shift_pairs(2, 1))
    low = lax.axis_index("zh") == 0
    pair = jnp.where(low, jnp.stack([permuted, other], axis=2), jnp.stack([other, permuted], axis=2))
    plane = lax.axis_size("x") * lax.axis_size("y")
    copies = jnp.broadcast_to(pair[:, :, None], pair.shape[:2] + (plane,) + pair.shape[2:])
    halves = 2
    span = width // halves
    stem_t = jnp.transpose(stem_tensor, (0, 2, 1, 3))
    open_t = open_tensor
    zl_count = lax.axis_size("zq") * lax.axis_size("zb")
    block_rows = row_count // (zl_count * 2)
    core = lax.axis_index("core")
    results = []
    previous = None
    for h in range(halves):
        part = copies[..., h * span:(h + 1) * span]
        if previous is not None:
            part, previous = lax.optimization_barrier((part, previous))
        gathered = lax.all_to_all(part, ("x", "y"), 2, 4, tiled=True)
        previous = gathered
        branch_t = gathered.reshape(slice_count, 2, -1, span)
        local_sum = contract(stem_t, branch_t, open_t, h)
        shaped = local_sum.reshape(2, zl_count, 2, block_rows, span)
        mine = lax.dynamic_index_in_dim(shaped, core, 2, keepdims=False)
        theirs = lax.dynamic_index_in_dim(shaped, 1 - core, 2, keepdims=False)
        mine = mine + lax.ppermute(theirs, "core", shift_pairs(2, 1))
        results.append(cuts_scatter(mine))
    result = jnp.concatenate(results, axis=-1)
    return jnp.transpose(result, (1, 0, 2)).reshape(1, block_rows, 2, width)


def solution(mesh):
    fine = split_mesh(mesh)
    spec = P(CUTS, STEM, None, None)
    return jax.shard_map(
        body,
        mesh=fine,
        in_specs=(spec, spec, spec, P(CUTS, None)),
        out_specs=P(STEM, CUTS, None, None),
        check_vma=False,
    )
```

```python
import jax
import jax.numpy as jnp
from jax import lax
from jax.experimental import pallas as pl
from jax.sharding import Mesh
from jax.sharding import PartitionSpec as P

CUTS = ("zl", "core")
STEM = ("zh", "x", "y")
ROW_TILE = 256


def split_mesh(mesh):
    devices = mesh.devices.reshape(8, 2, 2, 4, 4)
    return Mesh(devices, CUTS + STEM)


def shift_pairs(count, step):
    return [(i, (i + step) % count) for i in range(count)]


def ring_gather(block, axis):
    count = lax.axis_size(axis)
    from_left = lax.ppermute(block, axis, shift_pairs(count, 1))
    from_right = lax.ppermute(block, axis, shift_pairs(count, -1))
    half = block.shape[-1] // 2
    far_a = lax.ppermute(from_left[..., :half], axis, shift_pairs(count, 1))
    far_b = lax.ppermute(from_right[..., half:], axis, shift_pairs(count, -1))
    far = jnp.concatenate([far_a, far_b], axis=-1)
    return [block, from_right, far, from_left]


def permute_columns(block, order):
    width = block.shape[-1]
    one_hot = (lax.broadcasted_iota(jnp.int32, (width, width), 0) == order[None, :]).astype(block.dtype)
    flat = block.reshape(-1, width)
    moved = jnp.dot(flat, one_hot, preferred_element_type=jnp.float32)
    return moved.astype(block.dtype).reshape(block.shape)


def contract_kernel(s_ref, b_ref, o_ref, out_ref):
    f32 = jnp.float32
    for t in range(s_ref.shape[0]):
        sr = s_ref[t, 0]
        si = s_ref[t, 1]
        br = b_ref[t, 0]
        bi = b_ref[t, 1]
        pr = jnp.dot(sr, br, preferred_element_type=f32) - jnp.dot(si, bi, preferred_element_type=f32)
        pi = jnp.dot(sr, bi, preferred_element_type=f32) + jnp.dot(si, br, preferred_element_type=f32)
        o_r = o_ref[t, :, 0, :].astype(f32)
        o_i = o_ref[t, :, 1, :].astype(f32)
        re = pr * o_r - pi * o_i
        im = pr * o_i + pi * o_r
        if t == 0:
            out_ref[0] = re
            out_ref[1] = im
        else:
            out_ref[0] += re
            out_ref[1] += im


def contract(stem_t, branch_t, open_t, column_block):
    slices, _, rows, depth = stem_t.shape
    width = branch_t.shape[-1]
    tile = min(ROW_TILE, rows)
    flops = slices * 8 * rows * depth * width
    moved = 2 * (stem_t.size + branch_t.size) + 2 * slices * 2 * rows * width + 4 * 2 * rows * width
    return pl.pallas_call(
        contract_kernel,
        out_shape=jax.ShapeDtypeStruct((2, rows, width), jnp.float32),
        grid=(rows // tile,),
        in_specs=[
            pl.BlockSpec((slices, 2, tile, depth), lambda i: (0, 0, i, 0)),
            pl.BlockSpec((slices, 2, depth, width), lambda i: (0, 0, 0, 0)),
            pl.BlockSpec((slices, tile, 2, width), lambda i: (0, i, 0, column_block)),
        ],
        out_specs=pl.BlockSpec((2, tile, width), lambda i: (0, i, 0)),
        cost_estimate=pl.CostEstimate(flops=flops, bytes_accessed=moved, transcendentals=0),
    )(stem_t, branch_t, open_t)


def halving_scatter(blocks, axis):
    count = lax.axis_size(axis)
    me = lax.axis_index(axis)
    shaped = blocks.reshape((2,) + (2,) * 3 + blocks.shape[2:])
    for bit_pos in range(3):
        along = 3 - bit_pos
        bit = (me >> bit_pos) & 1
        keep = lax.dynamic_index_in_dim(shaped, bit, along, keepdims=False)
        send = lax.dynamic_index_in_dim(shaped, 1 - bit, along, keepdims=False)
        pairs = [(i, i ^ (1 << bit_pos)) for i in range(count)]
        shaped = keep + lax.ppermute(send, axis, pairs)
    return shaped


def body(stem_tensor, branch_tensor, open_tensor, open_order):
    slice_count, row_count, _, width = stem_tensor.shape
    permuted = jnp.stack([permute_columns(branch_tensor[t], open_order[t]) for t in range(slice_count)])
    permuted = jnp.transpose(permuted, (0, 2, 1, 3))
    other = lax.ppermute(permuted, "zh", shift_pairs(2, 1))
    low = lax.axis_index("zh") == 0
    pair = jnp.where(low, jnp.stack([permuted, other], axis=2), jnp.stack([other, permuted], axis=2))
    plane = lax.axis_size("x") * lax.axis_size("y")
    copies = jnp.broadcast_to(pair[:, :, None], pair.shape[:2] + (plane,) + pair.shape[2:])
    halves = 2
    span = width // halves
    stem_t = jnp.transpose(stem_tensor, (0, 2, 1, 3))
    open_t = open_tensor
    zl_count = lax.axis_size("zl")
    block_rows = row_count // (zl_count * 2)
    core = lax.axis_index("core")
    results = []
    previous = None
    for h in range(halves):
        part = copies[..., h * span:(h + 1) * span]
        if previous is not None:
            part, previous, stem_t = lax.optimization_barrier((part, previous, stem_t))
        gathered = lax.all_to_all(part, ("x", "y"), 2, 4, tiled=True)
        previous = gathered
        branch_t = gathered.reshape(slice_count, 2, -1, span)
        local_sum = contract(stem_t, branch_t, open_t, h)
        shaped = local_sum.reshape(2, zl_count, 2, block_rows, span)
        mine = lax.dynamic_index_in_dim(shaped, core, 2, keepdims=False)
        theirs = lax.dynamic_index_in_dim(shaped, 1 - core, 2, keepdims=False)
        mine = mine + lax.ppermute(theirs, "core", shift_pairs(2, 1))
        results.append(halving_scatter(mine, "zl"))
    result = jnp.concatenate(results, axis=-1)
    return jnp.transpose(result, (1, 0, 2)).reshape(1, block_rows, 2, width)


def solution(mesh):
    fine = split_mesh(mesh)
    spec = P(CUTS, STEM, None, None)
    return jax.shard_map(
        body,
        mesh=fine,
        in_specs=(spec, spec, spec, P(CUTS, None)),
        out_specs=P(STEM, CUTS, None, None),
        check_vma=False,
    )
```

```python
import jax
import jax.numpy as jnp
from jax import lax
from jax.experimental import pallas as pl
from jax.sharding import Mesh
from jax.sharding import PartitionSpec as P

CUTS = ("zl", "core")
STEM = ("zh", "x", "y")
ROW_TILE = 256


def split_mesh(mesh):
    devices = mesh.devices.reshape(8, 2, 2, 4, 4)
    return Mesh(devices, CUTS + STEM)


def shift_pairs(count, step):
    return [(i, (i + step) % count) for i in range(count)]


def ring_gather(block, axis):
    count = lax.axis_size(axis)
    from_left = lax.ppermute(block, axis, shift_pairs(count, 1))
    from_right = lax.ppermute(block, axis, shift_pairs(count, -1))
    half = block.shape[-1] // 2
    far_a = lax.ppermute(from_left[..., :half], axis, shift_pairs(count, 1))
    far_b = lax.ppermute(from_right[..., half:], axis, shift_pairs(count, -1))
    far = jnp.concatenate([far_a, far_b], axis=-1)
    return [block, from_right, far, from_left]


def permute_columns(block, order):
    width = block.shape[-1]
    one_hot = (lax.broadcasted_iota(jnp.int32, (width, width), 0) == order[None, :]).astype(block.dtype)
    flat = block.reshape(-1, width)
    moved = jnp.dot(flat, one_hot, preferred_element_type=jnp.float32)
    return moved.astype(block.dtype).reshape(block.shape)


def contract_kernel(s_ref, b_ref, o_ref, out_ref):
    f32 = jnp.float32
    for t in range(s_ref.shape[0]):
        sr = s_ref[t, 0]
        si = s_ref[t, 1]
        br = b_ref[t, 0]
        bi = b_ref[t, 1]
        pr = jnp.dot(sr, br, preferred_element_type=f32) - jnp.dot(si, bi, preferred_element_type=f32)
        pi = jnp.dot(sr, bi, preferred_element_type=f32) + jnp.dot(si, br, preferred_element_type=f32)
        o_r = o_ref[t, :, 0, :].astype(f32)
        o_i = o_ref[t, :, 1, :].astype(f32)
        re = pr * o_r - pi * o_i
        im = pr * o_i + pi * o_r
        if t == 0:
            out_ref[0] = re
            out_ref[1] = im
        else:
            out_ref[0] += re
            out_ref[1] += im


def contract(stem_t, branch_t, open_t, column_block):
    slices, _, rows, depth = stem_t.shape
    width = depth // 2
    tile = min(ROW_TILE, rows)
    flops = slices * 8 * rows * depth * width
    moved = 2 * (stem_t.size + branch_t.size // 2) + 2 * slices * 2 * rows * width + 4 * 2 * rows * width
    return pl.pallas_call(
        contract_kernel,
        out_shape=jax.ShapeDtypeStruct((2, rows, width), jnp.float32),
        grid=(rows // tile,),
        in_specs=[
            pl.BlockSpec((slices, 2, tile, depth), lambda i: (0, 0, i, 0)),
            pl.BlockSpec((slices, 2, depth, width), lambda i: (0, 0, 0, column_block)),
            pl.BlockSpec((slices, tile, 2, width), lambda i: (0, i, 0, column_block)),
        ],
        out_specs=pl.BlockSpec((2, tile, width), lambda i: (0, i, 0)),
        cost_estimate=pl.CostEstimate(flops=flops, bytes_accessed=moved, transcendentals=0),
    )(stem_t, branch_t, open_t)


def halving_scatter(blocks, axis):
    count = lax.axis_size(axis)
    me = lax.axis_index(axis)
    shaped = blocks.reshape((2,) + (2,) * 3 + blocks.shape[2:])
    for bit_pos in range(3):
        along = 3 - bit_pos
        bit = (me >> bit_pos) & 1
        keep = lax.dynamic_index_in_dim(shaped, bit, along, keepdims=False)
        send = lax.dynamic_index_in_dim(shaped, 1 - bit, along, keepdims=False)
        pairs = [(i, i ^ (1 << bit_pos)) for i in range(count)]
        shaped = keep + lax.ppermute(send, axis, pairs)
    return shaped


def body(stem_tensor, branch_tensor, open_tensor, open_order):
    slice_count, row_count, _, width = stem_tensor.shape
    permuted = jnp.stack([permute_columns(branch_tensor[t], open_order[t]) for t in range(slice_count)])
    permuted = jnp.transpose(permuted, (0, 2, 1, 3))
    other = lax.ppermute(permuted, "zh", shift_pairs(2, 1))
    low = lax.axis_index("zh") == 0
    pair = jnp.where(low, jnp.stack([permuted, other], axis=2), jnp.stack([other, permuted], axis=2))
    plane = lax.axis_size("x") * lax.axis_size("y")
    copies = jnp.broadcast_to(pair[:, :, None], pair.shape[:2] + (plane,) + pair.shape[2:])
    gathered = lax.all_to_all(copies, ("x", "y"), 2, 4, tiled=True)
    branch_t = gathered.reshape(slice_count, 2, -1, width)
    halves = 2
    span = width // halves
    stem_t = jnp.transpose(stem_tensor, (0, 2, 1, 3))
    open_t = open_tensor
    zl_count = lax.axis_size("zl")
    block_rows = row_count // (zl_count * 2)
    core = lax.axis_index("core")
    results = []
    for h in range(halves):
        local_sum = contract(stem_t, branch_t, open_t, h)
        shaped = local_sum.reshape(2, zl_count, 2, block_rows, span)
        mine = lax.dynamic_index_in_dim(shaped, core, 2, keepdims=False)
        theirs = lax.dynamic_index_in_dim(shaped, 1 - core, 2, keepdims=False)
        mine = mine + lax.ppermute(theirs, "core", shift_pairs(2, 1))
        results.append(halving_scatter(mine, "zl"))
    result = jnp.concatenate(results, axis=-1)
    return jnp.transpose(result, (1, 0, 2)).reshape(1, block_rows, 2, width)


def solution(mesh):
    fine = split_mesh(mesh)
    spec = P(CUTS, STEM, None, None)
    return jax.shard_map(
        body,
        mesh=fine,
        in_specs=(spec, spec, spec, P(CUTS, None)),
        out_specs=P(STEM, CUTS, None, None),
        check_vma=False,
    )
```

```python
import jax
import jax.numpy as jnp
from jax import lax
from jax.experimental import pallas as pl
from jax.sharding import Mesh
from jax.sharding import PartitionSpec as P

CUTS = ("zl", "core")
STEM = ("zh", "x", "y")
ROW_TILE = 256


def split_mesh(mesh):
    devices = mesh.devices.reshape(8, 2, 2, 4, 4)
    return Mesh(devices, CUTS + STEM)


def shift_pairs(count, step):
    return [(i, (i + step) % count) for i in range(count)]


def ring_gather(block, axis):
    count = lax.axis_size(axis)
    from_left = lax.ppermute(block, axis, shift_pairs(count, 1))
    from_right = lax.ppermute(block, axis, shift_pairs(count, -1))
    half = block.shape[-1] // 2
    far_a = lax.ppermute(from_left[..., :half], axis, shift_pairs(count, 1))
    far_b = lax.ppermute(from_right[..., half:], axis, shift_pairs(count, -1))
    far = jnp.concatenate([far_a, far_b], axis=-1)
    return [block, from_right, far, from_left]


def permute_columns(block, order):
    width = block.shape[-1]
    one_hot = (lax.broadcasted_iota(jnp.int32, (width, width), 0) == order[None, :]).astype(block.dtype)
    flat = block.reshape(-1, width)
    moved = jnp.dot(flat, one_hot, preferred_element_type=jnp.float32)
    return moved.astype(block.dtype).reshape(block.shape)


def contract_kernel(s_ref, b_ref, o_ref, out_ref):
    f32 = jnp.float32
    for t in range(s_ref.shape[0]):
        sr = s_ref[t, 0]
        si = s_ref[t, 1]
        br = b_ref[t, 0]
        bi = b_ref[t, 1]
        pr = jnp.dot(sr, br, preferred_element_type=f32) - jnp.dot(si, bi, preferred_element_type=f32)
        pi = jnp.dot(sr, bi, preferred_element_type=f32) + jnp.dot(si, br, preferred_element_type=f32)
        o_r = o_ref[t, :, 0, :].astype(f32)
        o_i = o_ref[t, :, 1, :].astype(f32)
        re = pr * o_r - pi * o_i
        im = pr * o_i + pi * o_r
        if t == 0:
            out_ref[0] = re
            out_ref[1] = im
        else:
            out_ref[0] += re
            out_ref[1] += im


def contract(stem_t, branch_t, open_t, column_block):
    slices, _, rows, depth = stem_t.shape
    width = depth // 2
    tile = min(ROW_TILE, rows)
    flops = slices * 8 * rows * depth * width
    moved = 2 * (stem_t.size + branch_t.size // 2) + 2 * slices * 2 * rows * width + 4 * 2 * rows * width
    return pl.pallas_call(
        contract_kernel,
        out_shape=jax.ShapeDtypeStruct((2, rows, width), jnp.float32),
        grid=(rows // tile,),
        in_specs=[
            pl.BlockSpec((slices, 2, tile, depth), lambda i: (0, 0, i, 0)),
            pl.BlockSpec((slices, 2, depth, width), lambda i: (0, 0, 0, column_block)),
            pl.BlockSpec((slices, tile, 2, width), lambda i: (0, i, 0, column_block)),
        ],
        out_specs=pl.BlockSpec((2, tile, width), lambda i: (0, i, 0)),
        cost_estimate=pl.CostEstimate(flops=flops, bytes_accessed=moved, transcendentals=0),
    )(stem_t, branch_t, open_t)


def halving_scatter(blocks, axis):
    count = lax.axis_size(axis)
    me = lax.axis_index(axis)
    shaped = blocks.reshape((2,) + (2,) * 3 + blocks.shape[2:])
    for bit_pos in range(3):
        along = 3 - bit_pos
        bit = (me >> bit_pos) & 1
        keep = lax.dynamic_index_in_dim(shaped, bit, along, keepdims=False)
        send = lax.dynamic_index_in_dim(shaped, 1 - bit, along, keepdims=False)
        pairs = [(i, i ^ (1 << bit_pos)) for i in range(count)]
        shaped = keep + lax.ppermute(send, axis, pairs)
    return shaped


def body(stem_tensor, branch_tensor, open_tensor, open_order):
    slice_count, row_count, _, width = stem_tensor.shape
    permuted = jnp.stack([permute_columns(branch_tensor[t], open_order[t]) for t in range(slice_count)])
    permuted = jnp.transpose(permuted, (0, 2, 1, 3))
    other = lax.ppermute(permuted, "zh", shift_pairs(2, 1))
    low = lax.axis_index("zh") == 0
    pair = jnp.where(low, jnp.stack([permuted, other], axis=2), jnp.stack([other, permuted], axis=2))
    plane = lax.axis_size("x") * lax.axis_size("y")
    copies = jnp.broadcast_to(pair[:, :, None], pair.shape[:2] + (plane,) + pair.shape[2:])
    gathered = lax.all_to_all(copies, ("x", "y"), 2, 4, tiled=True)
    branch_t = gathered.reshape(slice_count, 2, -1, width)
    halves = 2
    span = width // halves
    stem_t = jnp.transpose(stem_tensor, (0, 2, 1, 3))
    open_t = open_tensor
    zl_count = lax.axis_size("zl")
    block_rows = row_count // (zl_count * 2)
    core = lax.axis_index("core")
    results = []
    for h in range(halves):
        local_sum = contract(stem_t, branch_t, open_t, h)
        shaped = local_sum.reshape(2, zl_count, 2, block_rows, span)
        mine = lax.dynamic_index_in_dim(shaped, core, 2, keepdims=False)
        theirs = lax.dynamic_index_in_dim(shaped, 1 - core, 2, keepdims=False)
        mine = mine + lax.ppermute(theirs, "core", shift_pairs(2, 1))
        if h == 0:
            results.append(halving_scatter(mine, "zl"))
        else:
            summed = lax.psum_scatter(mine, "zl", scatter_dimension=1, tiled=True)
            results.append(summed.reshape(2, block_rows, span))
    result = jnp.concatenate(results, axis=-1)
    return jnp.transpose(result, (1, 0, 2)).reshape(1, block_rows, 2, width)


def solution(mesh):
    fine = split_mesh(mesh)
    spec = P(CUTS, STEM, None, None)
    return jax.shard_map(
        body,
        mesh=fine,
        in_specs=(spec, spec, spec, P(CUTS, None)),
        out_specs=P(STEM, CUTS, None, None),
        check_vma=False,
    )
```

```python
import jax
import jax.numpy as jnp
from jax import lax
from jax.experimental import pallas as pl
from jax.experimental.pallas import tpu as pltpu
from jax.sharding import Mesh
from jax.sharding import PartitionSpec as P

CUTS = ("zl", "core")
STEM = ("zh", "x", "y")
ROW_TILE = 256


def split_mesh(mesh):
    devices = mesh.devices.reshape(8, 2, 2, 4, 4)
    return Mesh(devices, CUTS + STEM)


def shift_pairs(count, step):
    return [(i, (i + step) % count) for i in range(count)]


def ring_gather(block, axis):
    count = lax.axis_size(axis)
    from_left = lax.ppermute(block, axis, shift_pairs(count, 1))
    from_right = lax.ppermute(block, axis, shift_pairs(count, -1))
    half = block.shape[-1] // 2
    far_a = lax.ppermute(from_left[..., :half], axis, shift_pairs(count, 1))
    far_b = lax.ppermute(from_right[..., half:], axis, shift_pairs(count, -1))
    far = jnp.concatenate([far_a, far_b], axis=-1)
    return [block, from_right, far, from_left]


def permute_columns(block, order):
    width = block.shape[-1]
    one_hot = (lax.broadcasted_iota(jnp.int32, (width, width), 0) == order[None, :]).astype(block.dtype)
    flat = block.reshape(-1, width)
    moved = jnp.dot(flat, one_hot, preferred_element_type=jnp.float32)
    return moved.astype(block.dtype).reshape(block.shape)


def contract_kernel(core_ref, s_ref, b_ref, o_ref, out_ref, acc_ref):
    f32 = jnp.float32
    for t in range(s_ref.shape[0]):
        sr = s_ref[t, 0]
        si = s_ref[t, 1]
        br = b_ref[t, 0]
        bi = b_ref[t, 1]
        pr = jnp.dot(sr, br, preferred_element_type=f32) - jnp.dot(si, bi, preferred_element_type=f32)
        pi = jnp.dot(sr, bi, preferred_element_type=f32) + jnp.dot(si, br, preferred_element_type=f32)
        o_r = o_ref[t, :, 0, :].astype(f32)
        o_i = o_ref[t, :, 1, :].astype(f32)
        re = pr * o_r - pi * o_i
        im = pr * o_i + pi * o_r
        if t == 0:
            acc_ref[0] = re
            acc_ref[1] = im
        else:
            acc_ref[0] += re
            acc_ref[1] += im
    core = core_ref[0]
    block = out_ref.shape[-2]
    for chip in range(out_ref.shape[2]):
        for slot in range(2):
            owner = core if slot == 0 else 1 - core
            start = pl.multiple_of((chip * 2 + owner) * block, block)
            out_ref[:, slot, chip] = acc_ref[:, pl.ds(start, block), :]


def contract(stem_t, branch_t, open_t, column_block, core, block_rows):
    slices, _, rows, depth = stem_t.shape
    width = branch_t.shape[-1]
    tile = min(ROW_TILE, rows)
    chips = rows // (2 * block_rows)
    per_tile = tile // (2 * block_rows)
    flops = slices * 8 * rows * depth * width
    moved = 2 * (stem_t.size + branch_t.size) + 2 * slices * 2 * rows * width + 4 * 2 * rows * width
    return pl.pallas_call(
        contract_kernel,
        out_shape=jax.ShapeDtypeStruct((2, 2, chips, block_rows, width), jnp.float32),
        grid_spec=pltpu.PrefetchScalarGridSpec(
            num_scalar_prefetch=1,
            grid=(rows // tile,),
            in_specs=[
                pl.BlockSpec((slices, 2, tile, depth), lambda i, c: (0, 0, i, 0)),
                pl.BlockSpec((slices, 2, depth, width), lambda i, c: (0, 0, 0, 0)),
                pl.BlockSpec((slices, tile, 2, width), lambda i, c: (0, i, 0, column_block)),
            ],
            out_specs=pl.BlockSpec((2, 2, per_tile, block_rows, width), lambda i, c: (0, 0, i, 0, 0)),
            scratch_shapes=[pltpu.VMEM((2, tile, width), jnp.float32)],
        ),
        cost_estimate=pl.CostEstimate(flops=flops, bytes_accessed=moved, transcendentals=0),
    )(core, stem_t, branch_t, open_t)


def halving_scatter(blocks, axis):
    count = lax.axis_size(axis)
    me = lax.axis_index(axis)
    shaped = blocks.reshape((2,) + (2,) * 3 + blocks.shape[2:])
    for bit_pos in range(3):
        along = 3 - bit_pos
        bit = (me >> bit_pos) & 1
        keep = lax.dynamic_index_in_dim(shaped, bit, along, keepdims=False)
        send = lax.dynamic_index_in_dim(shaped, 1 - bit, along, keepdims=False)
        pairs = [(i, i ^ (1 << bit_pos)) for i in range(count)]
        shaped = keep + lax.ppermute(send, axis, pairs)
    return shaped


def body(stem_tensor, branch_tensor, open_tensor, open_order):
    slice_count, row_count, _, width = stem_tensor.shape
    permuted = jnp.stack([permute_columns(branch_tensor[t], open_order[t]) for t in range(slice_count)])
    permuted = jnp.transpose(permuted, (0, 2, 1, 3))
    other = lax.ppermute(permuted, "zh", shift_pairs(2, 1))
    low = lax.axis_index("zh") == 0
    pair = jnp.where(low, jnp.stack([permuted, other], axis=2), jnp.stack([other, permuted], axis=2))
    plane = lax.axis_size("x") * lax.axis_size("y")
    copies = jnp.broadcast_to(pair[:, :, None], pair.shape[:2] + (plane,) + pair.shape[2:])
    halves = 2
    span = width // halves
    stem_t = jnp.transpose(stem_tensor, (0, 2, 1, 3))
    open_t = open_tensor
    zl_count = lax.axis_size("zl")
    block_rows = row_count // (zl_count * 2)
    core_index = jnp.reshape(lax.axis_index("core"), (1,)).astype(jnp.int32)
    results = []
    previous = None
    for h in range(halves):
        part = copies[..., h * span:(h + 1) * span]
        if previous is not None:
            part, previous = lax.optimization_barrier((part, previous))
        gathered = lax.all_to_all(part, ("x", "y"), 2, 4, tiled=True)
        previous = gathered
        branch_t = gathered.reshape(slice_count, 2, -1, span)
        local_sum = contract(stem_t, branch_t, open_t, h, core_index, block_rows)
        mine = local_sum[:, 0] + lax.ppermute(local_sum[:, 1], "core", shift_pairs(2, 1))
        results.append(halving_scatter(mine, "zl"))
    result = jnp.concatenate(results, axis=-1)
    return jnp.transpose(result, (1, 0, 2)).reshape(1, block_rows, 2, width)


def solution(mesh):
    fine = split_mesh(mesh)
    spec = P(CUTS, STEM, None, None)
    return jax.shard_map(
        body,
        mesh=fine,
        in_specs=(spec, spec, spec, P(CUTS, None)),
        out_specs=P(STEM, CUTS, None, None),
        check_vma=False,
    )
```

```python
import jax
import jax.numpy as jnp
from jax import lax
from jax.experimental import pallas as pl
from jax.sharding import Mesh
from jax.sharding import PartitionSpec as P

CUTS = ("zl", "core")
STEM = ("zh", "x", "y")
ROW_TILE = 256


def split_mesh(mesh):
    devices = mesh.devices.reshape(8, 2, 2, 4, 4)
    return Mesh(devices, CUTS + STEM)


def shift_pairs(count, step):
    return [(i, (i + step) % count) for i in range(count)]


def ring_gather(block, axis):
    count = lax.axis_size(axis)
    from_left = lax.ppermute(block, axis, shift_pairs(count, 1))
    from_right = lax.ppermute(block, axis, shift_pairs(count, -1))
    half = block.shape[-1] // 2
    far_a = lax.ppermute(from_left[..., :half], axis, shift_pairs(count, 1))
    far_b = lax.ppermute(from_right[..., half:], axis, shift_pairs(count, -1))
    far = jnp.concatenate([far_a, far_b], axis=-1)
    return [block, from_right, far, from_left]


def permute_columns(block, order):
    width = block.shape[-1]
    one_hot = (lax.broadcasted_iota(jnp.int32, (width, width), 0) == order[None, :]).astype(block.dtype)
    flat = block.reshape(-1, width)
    moved = jnp.dot(flat, one_hot, preferred_element_type=jnp.float32)
    return moved.astype(block.dtype).reshape(block.shape)


def contract_kernel(s_ref, b_ref, o_ref, out_ref):
    f32 = jnp.float32
    for t in range(s_ref.shape[0]):
        sr = s_ref[t, 0]
        si = s_ref[t, 1]
        br = b_ref[t, 0]
        bi = b_ref[t, 1]
        pr = jnp.dot(sr, br, preferred_element_type=f32) - jnp.dot(si, bi, preferred_element_type=f32)
        pi = jnp.dot(sr, bi, preferred_element_type=f32) + jnp.dot(si, br, preferred_element_type=f32)
        o_r = o_ref[t, :, 0, :].astype(f32)
        o_i = o_ref[t, :, 1, :].astype(f32)
        re = pr * o_r - pi * o_i
        im = pr * o_i + pi * o_r
        if t == 0:
            out_ref[0] = re
            out_ref[1] = im
        else:
            out_ref[0] += re
            out_ref[1] += im


def contract(stem_t, branch_t, open_t, column_block):
    slices, _, rows, depth = stem_t.shape
    width = branch_t.shape[-1]
    tile = min(ROW_TILE, rows)
    flops = slices * 8 * rows * depth * width
    moved = 2 * (stem_t.size + branch_t.size) + 2 * slices * 2 * rows * width + 4 * 2 * rows * width
    return pl.pallas_call(
        contract_kernel,
        out_shape=jax.ShapeDtypeStruct((2, rows, width), jnp.float32),
        grid=(rows // tile,),
        in_specs=[
            pl.BlockSpec((slices, 2, tile, depth), lambda i: (0, 0, i, 0)),
            pl.BlockSpec((slices, 2, depth, width), lambda i: (0, 0, 0, 0)),
            pl.BlockSpec((slices, tile, 2, width), lambda i: (0, i, 0, column_block)),
        ],
        out_specs=pl.BlockSpec((2, tile, width), lambda i: (0, i, 0)),
        cost_estimate=pl.CostEstimate(flops=flops, bytes_accessed=moved, transcendentals=0),
    )(stem_t, branch_t, open_t)


def halving_scatter(blocks, axis):
    count = lax.axis_size(axis)
    me = lax.axis_index(axis)
    shaped = blocks.reshape((2,) + (2,) * 3 + blocks.shape[2:])
    for bit_pos in range(3):
        along = 3 - bit_pos
        bit = (me >> bit_pos) & 1
        keep = lax.dynamic_index_in_dim(shaped, bit, along, keepdims=False)
        send = lax.dynamic_index_in_dim(shaped, 1 - bit, along, keepdims=False)
        pairs = [(i, i ^ (1 << bit_pos)) for i in range(count)]
        shaped = keep + lax.ppermute(send, axis, pairs)
    return shaped


def body(stem_tensor, branch_tensor, open_tensor, open_order):
    slice_count, row_count, _, width = stem_tensor.shape
    permuted = jnp.stack([permute_columns(branch_tensor[t], open_order[t]) for t in range(slice_count)])
    permuted = jnp.transpose(permuted, (0, 2, 1, 3))
    other = lax.ppermute(permuted, "zh", shift_pairs(2, 1))
    low = lax.axis_index("zh") == 0
    pair = jnp.where(low, jnp.stack([permuted, other], axis=2), jnp.stack([other, permuted], axis=2))
    plane = lax.axis_size("x") * lax.axis_size("y")
    copies = jnp.broadcast_to(pair[:, :, None], pair.shape[:2] + (plane,) + pair.shape[2:])
    halves = 4
    span = width // halves
    stem_t = jnp.transpose(stem_tensor, (0, 2, 1, 3))
    open_t = open_tensor
    zl_count = lax.axis_size("zl")
    block_rows = row_count // (zl_count * 2)
    core = lax.axis_index("core")
    results = []
    previous = None
    for h in range(halves):
        part = copies[..., h * span:(h + 1) * span]
        if previous is not None:
            part, previous = lax.optimization_barrier((part, previous))
        gathered = lax.all_to_all(part, ("x", "y"), 2, 4, tiled=True)
        previous = gathered
        branch_t = gathered.reshape(slice_count, 2, -1, span)
        local_sum = contract(stem_t, branch_t, open_t, h)
        shaped = local_sum.reshape(2, zl_count, 2, block_rows, span)
        mine = lax.dynamic_index_in_dim(shaped, core, 2, keepdims=False)
        theirs = lax.dynamic_index_in_dim(shaped, 1 - core, 2, keepdims=False)
        mine = mine + lax.ppermute(theirs, "core", shift_pairs(2, 1))
        results.append(halving_scatter(mine, "zl"))
    result = jnp.concatenate(results, axis=-1)
    return jnp.transpose(result, (1, 0, 2)).reshape(1, block_rows, 2, width)


def solution(mesh):
    fine = split_mesh(mesh)
    spec = P(CUTS, STEM, None, None)
    return jax.shard_map(
        body,
        mesh=fine,
        in_specs=(spec, spec, spec, P(CUTS, None)),
        out_specs=P(STEM, CUTS, None, None),
        check_vma=False,
    )
```

```python
import jax
import jax.numpy as jnp
from jax import lax
from jax.experimental import pallas as pl
from jax.sharding import Mesh
from jax.sharding import PartitionSpec as P

CUTS = ("zl", "core")
STEM = ("zh", "x", "y")
ROW_TILE = 256


def split_mesh(mesh):
    devices = mesh.devices.reshape(8, 2, 2, 4, 4)
    return Mesh(devices, CUTS + STEM)


def shift_pairs(count, step):
    return [(i, (i + step) % count) for i in range(count)]


def ring_gather(block, axis):
    count = lax.axis_size(axis)
    from_left = lax.ppermute(block, axis, shift_pairs(count, 1))
    from_right = lax.ppermute(block, axis, shift_pairs(count, -1))
    half = block.shape[-1] // 2
    far_a = lax.ppermute(from_left[..., :half], axis, shift_pairs(count, 1))
    far_b = lax.ppermute(from_right[..., half:], axis, shift_pairs(count, -1))
    far = jnp.concatenate([far_a, far_b], axis=-1)
    return [block, from_right, far, from_left]


def permute_columns(block, order):
    width = block.shape[-1]
    one_hot = (lax.broadcasted_iota(jnp.int32, (width, width), 0) == order[None, :]).astype(block.dtype)
    flat = block.reshape(-1, width)
    moved = jnp.dot(flat, one_hot, preferred_element_type=jnp.float32)
    return moved.astype(block.dtype).reshape(block.shape)


def contract_kernel(s_ref, b_ref, o_ref, out_ref):
    f32 = jnp.float32
    for t in range(s_ref.shape[0]):
        sr = s_ref[t, 0]
        si = s_ref[t, 1]
        br = b_ref[t, 0]
        bi = b_ref[t, 1]
        pr = jnp.dot(sr, br, preferred_element_type=f32) - jnp.dot(si, bi, preferred_element_type=f32)
        pi = jnp.dot(sr, bi, preferred_element_type=f32) + jnp.dot(si, br, preferred_element_type=f32)
        o_r = o_ref[t, :, 0, :].astype(f32)
        o_i = o_ref[t, :, 1, :].astype(f32)
        re = pr * o_r - pi * o_i
        im = pr * o_i + pi * o_r
        if t == 0:
            out_ref[0] = re
            out_ref[1] = im
        else:
            out_ref[0] += re
            out_ref[1] += im


def contract(stem_t, branch_t, open_t, column_block):
    slices, _, rows, depth = stem_t.shape
    width = branch_t.shape[-1]
    tile = min(ROW_TILE, rows)
    flops = slices * 8 * rows * depth * width
    moved = 2 * (stem_t.size + branch_t.size) + 2 * slices * 2 * rows * width + 4 * 2 * rows * width
    return pl.pallas_call(
        contract_kernel,
        out_shape=jax.ShapeDtypeStruct((2, rows, width), jnp.float32),
        grid=(rows // tile,),
        in_specs=[
            pl.BlockSpec((slices, 2, tile, depth), lambda i: (0, 0, i, 0)),
            pl.BlockSpec((slices, 2, depth, width), lambda i: (0, 0, 0, 0)),
            pl.BlockSpec((slices, tile, 2, width), lambda i: (0, i, 0, column_block)),
        ],
        out_specs=pl.BlockSpec((2, tile, width), lambda i: (0, i, 0)),
        cost_estimate=pl.CostEstimate(flops=flops, bytes_accessed=moved, transcendentals=0),
    )(stem_t, branch_t, open_t)


def halving_scatter(blocks, axis):
    count = lax.axis_size(axis)
    me = lax.axis_index(axis)
    shaped = blocks.reshape((2,) + (2,) * 3 + blocks.shape[2:])
    for bit_pos in range(3):
        along = 3 - bit_pos
        bit = (me >> bit_pos) & 1
        keep = lax.dynamic_index_in_dim(shaped, bit, along, keepdims=False)
        send = lax.dynamic_index_in_dim(shaped, 1 - bit, along, keepdims=False)
        pairs = [(i, i ^ (1 << bit_pos)) for i in range(count)]
        shaped = keep + lax.ppermute(send, axis, pairs)
    return shaped


def body(stem_tensor, branch_tensor, open_tensor, open_order):
    slice_count, row_count, _, width = stem_tensor.shape
    permuted = jnp.stack([permute_columns(branch_tensor[t], open_order[t]) for t in range(slice_count)])
    permuted = jnp.transpose(permuted, (0, 2, 1, 3))
    other = lax.ppermute(permuted, "zh", shift_pairs(2, 1))
    low = lax.axis_index("zh") == 0
    pair = jnp.where(low, jnp.stack([permuted, other], axis=2), jnp.stack([other, permuted], axis=2))
    plane = lax.axis_size("x") * lax.axis_size("y")
    copies = jnp.broadcast_to(pair[:, :, None], pair.shape[:2] + (plane,) + pair.shape[2:])
    spans = [3 * width // 4, width // 4]
    stem_t = jnp.transpose(stem_tensor, (0, 2, 1, 3))
    open_t = open_tensor
    zl_count = lax.axis_size("zl")
    block_rows = row_count // (zl_count * 2)
    core = lax.axis_index("core")
    results = []
    previous = None
    offset = 0
    for span in spans:
        part = copies[..., offset:offset + span]
        if previous is not None:
            part, previous = lax.optimization_barrier((part, previous))
        gathered = lax.all_to_all(part, ("x", "y"), 2, 4, tiled=True)
        previous = gathered
        branch_t = gathered.reshape(slice_count, 2, -1, span)
        column_block = offset // span
        offset += span
        local_sum = contract(stem_t, branch_t, open_t, column_block)
        shaped = local_sum.reshape(2, zl_count, 2, block_rows, span)
        mine = lax.dynamic_index_in_dim(shaped, core, 2, keepdims=False)
        theirs = lax.dynamic_index_in_dim(shaped, 1 - core, 2, keepdims=False)
        mine = mine + lax.ppermute(theirs, "core", shift_pairs(2, 1))
        results.append(halving_scatter(mine, "zl"))
    result = jnp.concatenate(results, axis=-1)
    return jnp.transpose(result, (1, 0, 2)).reshape(1, block_rows, 2, width)


def solution(mesh):
    fine = split_mesh(mesh)
    spec = P(CUTS, STEM, None, None)
    return jax.shard_map(
        body,
        mesh=fine,
        in_specs=(spec, spec, spec, P(CUTS, None)),
        out_specs=P(STEM, CUTS, None, None),
        check_vma=False,
    )
```

```python
import jax
import jax.numpy as jnp
from jax import lax
from jax.experimental import pallas as pl
from jax.sharding import Mesh
from jax.sharding import PartitionSpec as P

CUTS = ("zl", "core")
STEM = ("zh", "x", "y")
ROW_TILE = 256


def split_mesh(mesh):
    devices = mesh.devices.reshape(8, 2, 2, 4, 4)
    return Mesh(devices, CUTS + STEM)


def shift_pairs(count, step):
    return [(i, (i + step) % count) for i in range(count)]


def ring_gather(block, axis):
    count = lax.axis_size(axis)
    from_left = lax.ppermute(block, axis, shift_pairs(count, 1))
    from_right = lax.ppermute(block, axis, shift_pairs(count, -1))
    half = block.shape[-1] // 2
    far_a = lax.ppermute(from_left[..., :half], axis, shift_pairs(count, 1))
    far_b = lax.ppermute(from_right[..., half:], axis, shift_pairs(count, -1))
    far = jnp.concatenate([far_a, far_b], axis=-1)
    return [block, from_right, far, from_left]


def permute_columns(block, order):
    width = block.shape[-1]
    one_hot = (lax.broadcasted_iota(jnp.int32, (width, width), 0) == order[None, :]).astype(block.dtype)
    flat = block.reshape(-1, width)
    moved = jnp.dot(flat, one_hot, preferred_element_type=jnp.float32)
    return moved.astype(block.dtype).reshape(block.shape)


def contract_kernel(s_ref, b_ref, o_ref, out_ref):
    f32 = jnp.float32
    for t in range(s_ref.shape[0]):
        sr = s_ref[t, 0]
        si = s_ref[t, 1]
        br = b_ref[t, 0]
        bi = b_ref[t, 1]
        pr = jnp.dot(sr, br, preferred_element_type=f32) - jnp.dot(si, bi, preferred_element_type=f32)
        pi = jnp.dot(sr, bi, preferred_element_type=f32) + jnp.dot(si, br, preferred_element_type=f32)
        o_r = o_ref[t, :, 0, :].astype(f32)
        o_i = o_ref[t, :, 1, :].astype(f32)
        re = pr * o_r - pi * o_i
        im = pr * o_i + pi * o_r
        if t == 0:
            out_ref[0] = re
            out_ref[1] = im
        else:
            out_ref[0] += re
            out_ref[1] += im


def contract(stem_t, branch_t, open_t, column_block):
    slices, _, rows, depth = stem_t.shape
    width = branch_t.shape[-1]
    tile = min(ROW_TILE, rows)
    flops = slices * 8 * rows * depth * width
    moved = 2 * (stem_t.size + branch_t.size) + 2 * slices * 2 * rows * width + 4 * 2 * rows * width
    return pl.pallas_call(
        contract_kernel,
        out_shape=jax.ShapeDtypeStruct((2, rows, width), jnp.float32),
        grid=(rows // tile,),
        in_specs=[
            pl.BlockSpec((slices, 2, tile, depth), lambda i: (0, 0, i, 0)),
            pl.BlockSpec((slices, 2, depth, width), lambda i: (0, 0, 0, 0)),
            pl.BlockSpec((slices, tile, 2, width), lambda i: (0, i, 0, column_block)),
        ],
        out_specs=pl.BlockSpec((2, tile, width), lambda i: (0, i, 0)),
        cost_estimate=pl.CostEstimate(flops=flops, bytes_accessed=moved, transcendentals=0),
    )(stem_t, branch_t, open_t)


def halving_scatter(blocks, axis):
    count = lax.axis_size(axis)
    me = lax.axis_index(axis)
    shaped = blocks.reshape((2,) + (2,) * 3 + blocks.shape[2:])
    for bit_pos in range(3):
        along = 3 - bit_pos
        bit = (me >> bit_pos) & 1
        keep = lax.dynamic_index_in_dim(shaped, bit, along, keepdims=False)
        send = lax.dynamic_index_in_dim(shaped, 1 - bit, along, keepdims=False)
        pairs = [(i, i ^ (1 << bit_pos)) for i in range(count)]
        shaped = keep + lax.ppermute(send, axis, pairs)
    return shaped


def body(stem_tensor, branch_tensor, open_tensor, open_order):
    slice_count, row_count, _, width = stem_tensor.shape
    other_raw = lax.ppermute(branch_tensor, "zh", shift_pairs(2, 1))

    def permuted_of(shard):
        moved = jnp.stack([permute_columns(shard[t], open_order[t]) for t in range(slice_count)])
        return jnp.transpose(moved, (0, 2, 1, 3))

    permuted = permuted_of(branch_tensor)
    other = permuted_of(other_raw)
    low = lax.axis_index("zh") == 0
    pair = jnp.where(low, jnp.stack([permuted, other], axis=2), jnp.stack([other, permuted], axis=2))
    plane = lax.axis_size("x") * lax.axis_size("y")
    copies = jnp.broadcast_to(pair[:, :, None], pair.shape[:2] + (plane,) + pair.shape[2:])
    halves = 2
    span = width // halves
    stem_t = jnp.transpose(stem_tensor, (0, 2, 1, 3))
    open_t = open_tensor
    zl_count = lax.axis_size("zl")
    block_rows = row_count // (zl_count * 2)
    core = lax.axis_index("core")
    results = []
    previous = None
    for h in range(halves):
        part = copies[..., h * span:(h + 1) * span]
        if previous is not None:
            part, previous = lax.optimization_barrier((part, previous))
        gathered = lax.all_to_all(part, ("x", "y"), 2, 4, tiled=True)
        previous = gathered
        branch_t = gathered.reshape(slice_count, 2, -1, span)
        local_sum = contract(stem_t, branch_t, open_t, h)
        shaped = local_sum.reshape(2, zl_count, 2, block_rows, span)
        mine = lax.dynamic_index_in_dim(shaped, core, 2, keepdims=False)
        theirs = lax.dynamic_index_in_dim(shaped, 1 - core, 2, keepdims=False)
        mine = mine + lax.ppermute(theirs, "core", shift_pairs(2, 1))
        results.append(halving_scatter(mine, "zl"))
    result = jnp.concatenate(results, axis=-1)
    return jnp.transpose(result, (1, 0, 2)).reshape(1, block_rows, 2, width)


def solution(mesh):
    fine = split_mesh(mesh)
    spec = P(CUTS, STEM, None, None)
    return jax.shard_map(
        body,
        mesh=fine,
        in_specs=(spec, spec, spec, P(CUTS, None)),
        out_specs=P(STEM, CUTS, None, None),
        check_vma=False,
    )
```

```python
import jax
import jax.numpy as jnp
from jax import lax
from jax.experimental import pallas as pl
from jax.sharding import Mesh
from jax.sharding import PartitionSpec as P

CUTS = ("zl", "core")
STEM = ("zh", "x", "y")
ROW_TILE = 128


def split_mesh(mesh):
    devices = mesh.devices.reshape(8, 2, 2, 4, 4)
    return Mesh(devices, CUTS + STEM)


def shift_pairs(count, step):
    return [(i, (i + step) % count) for i in range(count)]


def ring_gather(block, axis):
    count = lax.axis_size(axis)
    from_left = lax.ppermute(block, axis, shift_pairs(count, 1))
    from_right = lax.ppermute(block, axis, shift_pairs(count, -1))
    half = block.shape[-1] // 2
    far_a = lax.ppermute(from_left[..., :half], axis, shift_pairs(count, 1))
    far_b = lax.ppermute(from_right[..., half:], axis, shift_pairs(count, -1))
    far = jnp.concatenate([far_a, far_b], axis=-1)
    return [block, from_right, far, from_left]


def permute_columns(block, order):
    width = block.shape[-1]
    one_hot = (lax.broadcasted_iota(jnp.int32, (width, width), 0) == order[None, :]).astype(block.dtype)
    flat = block.reshape(-1, width)
    moved = jnp.dot(flat, one_hot, preferred_element_type=jnp.float32)
    return moved.astype(block.dtype).reshape(block.shape)


def contract_kernel(s_ref, b_ref, o_ref, out_ref):
    f32 = jnp.float32
    for t in range(s_ref.shape[0]):
        sr = s_ref[t, 0]
        si = s_ref[t, 1]
        br = b_ref[t, 0]
        bi = b_ref[t, 1]
        pr = jnp.dot(sr, br, preferred_element_type=f32) - jnp.dot(si, bi, preferred_element_type=f32)
        pi = jnp.dot(sr, bi, preferred_element_type=f32) + jnp.dot(si, br, preferred_element_type=f32)
        o_r = o_ref[t, :, 0, :].astype(f32)
        o_i = o_ref[t, :, 1, :].astype(f32)
        re = pr * o_r - pi * o_i
        im = pr * o_i + pi * o_r
        if t == 0:
            out_ref[0] = re
            out_ref[1] = im
        else:
            out_ref[0] += re
            out_ref[1] += im


def contract(stem_t, branch_t, open_t, column_block):
    slices, _, rows, depth = stem_t.shape
    width = branch_t.shape[-1]
    tile = min(ROW_TILE, rows)
    flops = slices * 8 * rows * depth * width
    moved = 2 * (stem_t.size + branch_t.size) + 2 * slices * 2 * rows * width + 4 * 2 * rows * width
    return pl.pallas_call(
        contract_kernel,
        out_shape=jax.ShapeDtypeStruct((2, rows, width), jnp.float32),
        grid=(rows // tile,),
        in_specs=[
            pl.BlockSpec((slices, 2, tile, depth), lambda i: (0, 0, i, 0)),
            pl.BlockSpec((slices, 2, depth, width), lambda i: (0, 0, 0, 0)),
            pl.BlockSpec((slices, tile, 2, width), lambda i: (0, i, 0, column_block)),
        ],
        out_specs=pl.BlockSpec((2, tile, width), lambda i: (0, i, 0)),
        cost_estimate=pl.CostEstimate(flops=flops, bytes_accessed=moved, transcendentals=0),
    )(stem_t, branch_t, open_t)


def halving_scatter(blocks, axis):
    count = lax.axis_size(axis)
    me = lax.axis_index(axis)
    shaped = blocks.reshape((2,) + (2,) * 3 + blocks.shape[2:])
    for bit_pos in range(3):
        along = 3 - bit_pos
        bit = (me >> bit_pos) & 1
        keep = lax.dynamic_index_in_dim(shaped, bit, along, keepdims=False)
        send = lax.dynamic_index_in_dim(shaped, 1 - bit, along, keepdims=False)
        pairs = [(i, i ^ (1 << bit_pos)) for i in range(count)]
        shaped = keep + lax.ppermute(send, axis, pairs)
    return shaped


def body(stem_tensor, branch_tensor, open_tensor, open_order):
    slice_count, row_count, _, width = stem_tensor.shape
    other_raw = lax.ppermute(branch_tensor, "zh", shift_pairs(2, 1))

    def permuted_of(shard):
        moved = jnp.stack([permute_columns(shard[t], open_order[t]) for t in range(slice_count)])
        return jnp.transpose(moved, (0, 2, 1, 3))

    permuted = permuted_of(branch_tensor)
    other = permuted_of(other_raw)
    low = lax.axis_index("zh") == 0
    pair = jnp.where(low, jnp.stack([permuted, other], axis=2), jnp.stack([other, permuted], axis=2))
    plane = lax.axis_size("x") * lax.axis_size("y")
    copies = jnp.broadcast_to(pair[:, :, None], pair.shape[:2] + (plane,) + pair.shape[2:])
    halves = 2
    span = width // halves
    stem_t = jnp.transpose(stem_tensor, (0, 2, 1, 3))
    open_t = open_tensor
    zl_count = lax.axis_size("zl")
    block_rows = row_count // (zl_count * 2)
    core = lax.axis_index("core")
    results = []
    previous = None
    for h in range(halves):
        part = copies[..., h * span:(h + 1) * span]
        if previous is not None:
            part, previous = lax.optimization_barrier((part, previous))
        gathered = lax.all_to_all(part, ("x", "y"), 2, 4, tiled=True)
        previous = gathered
        branch_t = gathered.reshape(slice_count, 2, -1, span)
        local_sum = contract(stem_t, branch_t, open_t, h)
        shaped = local_sum.reshape(2, zl_count, 2, block_rows, span)
        mine = lax.dynamic_index_in_dim(shaped, core, 2, keepdims=False)
        theirs = lax.dynamic_index_in_dim(shaped, 1 - core, 2, keepdims=False)
        mine = mine + lax.ppermute(theirs, "core", shift_pairs(2, 1))
        results.append(halving_scatter(mine, "zl"))
    result = jnp.concatenate(results, axis=-1)
    return jnp.transpose(result, (1, 0, 2)).reshape(1, block_rows, 2, width)


def solution(mesh):
    fine = split_mesh(mesh)
    spec = P(CUTS, STEM, None, None)
    return jax.shard_map(
        body,
        mesh=fine,
        in_specs=(spec, spec, spec, P(CUTS, None)),
        out_specs=P(STEM, CUTS, None, None),
        check_vma=False,
    )
```

```python
import jax
import jax.numpy as jnp
from jax import lax
from jax.experimental import pallas as pl
from jax.sharding import Mesh
from jax.sharding import PartitionSpec as P

CUTS = ("zl", "core")
STEM = ("zh", "x", "y")
ROW_TILE = 512


def split_mesh(mesh):
    devices = mesh.devices.reshape(8, 2, 2, 4, 4)
    return Mesh(devices, CUTS + STEM)


def shift_pairs(count, step):
    return [(i, (i + step) % count) for i in range(count)]


def ring_gather(block, axis):
    count = lax.axis_size(axis)
    from_left = lax.ppermute(block, axis, shift_pairs(count, 1))
    from_right = lax.ppermute(block, axis, shift_pairs(count, -1))
    half = block.shape[-1] // 2
    far_a = lax.ppermute(from_left[..., :half], axis, shift_pairs(count, 1))
    far_b = lax.ppermute(from_right[..., half:], axis, shift_pairs(count, -1))
    far = jnp.concatenate([far_a, far_b], axis=-1)
    return [block, from_right, far, from_left]


def permute_columns(block, order):
    width = block.shape[-1]
    one_hot = (lax.broadcasted_iota(jnp.int32, (width, width), 0) == order[None, :]).astype(block.dtype)
    flat = block.reshape(-1, width)
    moved = jnp.dot(flat, one_hot, preferred_element_type=jnp.float32)
    return moved.astype(block.dtype).reshape(block.shape)


def contract_kernel(s_ref, b_ref, o_ref, out_ref):
    f32 = jnp.float32
    for t in range(s_ref.shape[0]):
        sr = s_ref[t, 0]
        si = s_ref[t, 1]
        br = b_ref[t, 0]
        bi = b_ref[t, 1]
        pr = jnp.dot(sr, br, preferred_element_type=f32) - jnp.dot(si, bi, preferred_element_type=f32)
        pi = jnp.dot(sr, bi, preferred_element_type=f32) + jnp.dot(si, br, preferred_element_type=f32)
        o_r = o_ref[t, :, 0, :].astype(f32)
        o_i = o_ref[t, :, 1, :].astype(f32)
        re = pr * o_r - pi * o_i
        im = pr * o_i + pi * o_r
        if t == 0:
            out_ref[0] = re
            out_ref[1] = im
        else:
            out_ref[0] += re
            out_ref[1] += im


def contract(stem_t, branch_t, open_t, column_block):
    slices, _, rows, depth = stem_t.shape
    width = branch_t.shape[-1]
    tile = min(ROW_TILE, rows)
    flops = slices * 8 * rows * depth * width
    moved = 2 * (stem_t.size + branch_t.size) + 2 * slices * 2 * rows * width + 4 * 2 * rows * width
    return pl.pallas_call(
        contract_kernel,
        out_shape=jax.ShapeDtypeStruct((2, rows, width), jnp.float32),
        grid=(rows // tile,),
        in_specs=[
            pl.BlockSpec((slices, 2, tile, depth), lambda i: (0, 0, i, 0)),
            pl.BlockSpec((slices, 2, depth, width), lambda i: (0, 0, 0, 0)),
            pl.BlockSpec((slices, tile, 2, width), lambda i: (0, i, 0, column_block)),
        ],
        out_specs=pl.BlockSpec((2, tile, width), lambda i: (0, i, 0)),
        cost_estimate=pl.CostEstimate(flops=flops, bytes_accessed=moved, transcendentals=0),
    )(stem_t, branch_t, open_t)


def halving_scatter(blocks, axis):
    count = lax.axis_size(axis)
    me = lax.axis_index(axis)
    shaped = blocks.reshape((2,) + (2,) * 3 + blocks.shape[2:])
    for bit_pos in range(3):
        along = 3 - bit_pos
        bit = (me >> bit_pos) & 1
        keep = lax.dynamic_index_in_dim(shaped, bit, along, keepdims=False)
        send = lax.dynamic_index_in_dim(shaped, 1 - bit, along, keepdims=False)
        pairs = [(i, i ^ (1 << bit_pos)) for i in range(count)]
        shaped = keep + lax.ppermute(send, axis, pairs)
    return shaped


def body(stem_tensor, branch_tensor, open_tensor, open_order):
    slice_count, row_count, _, width = stem_tensor.shape
    other_raw = lax.ppermute(branch_tensor, "zh", shift_pairs(2, 1))

    def permuted_of(shard):
        moved = jnp.stack([permute_columns(shard[t], open_order[t]) for t in range(slice_count)])
        return jnp.transpose(moved, (0, 2, 1, 3))

    permuted = permuted_of(branch_tensor)
    other = permuted_of(other_raw)
    low = lax.axis_index("zh") == 0
    pair = jnp.where(low, jnp.stack([permuted, other], axis=2), jnp.stack([other, permuted], axis=2))
    plane = lax.axis_size("x") * lax.axis_size("y")
    copies = jnp.broadcast_to(pair[:, :, None], pair.shape[:2] + (plane,) + pair.shape[2:])
    halves = 2
    span = width // halves
    stem_t = jnp.transpose(stem_tensor, (0, 2, 1, 3))
    open_t = open_tensor
    zl_count = lax.axis_size("zl")
    block_rows = row_count // (zl_count * 2)
    core = lax.axis_index("core")
    results = []
    previous = None
    for h in range(halves):
        part = copies[..., h * span:(h + 1) * span]
        if previous is not None:
            part, previous = lax.optimization_barrier((part, previous))
        gathered = lax.all_to_all(part, ("x", "y"), 2, 4, tiled=True)
        previous = gathered
        branch_t = gathered.reshape(slice_count, 2, -1, span)
        local_sum = contract(stem_t, branch_t, open_t, h)
        shaped = local_sum.reshape(2, zl_count, 2, block_rows, span)
        mine = lax.dynamic_index_in_dim(shaped, core, 2, keepdims=False)
        theirs = lax.dynamic_index_in_dim(shaped, 1 - core, 2, keepdims=False)
        mine = mine + lax.ppermute(theirs, "core", shift_pairs(2, 1))
        results.append(halving_scatter(mine, "zl"))
    result = jnp.concatenate(results, axis=-1)
    return jnp.transpose(result, (1, 0, 2)).reshape(1, block_rows, 2, width)


def solution(mesh):
    fine = split_mesh(mesh)
    spec = P(CUTS, STEM, None, None)
    return jax.shard_map(
        body,
        mesh=fine,
        in_specs=(spec, spec, spec, P(CUTS, None)),
        out_specs=P(STEM, CUTS, None, None),
        check_vma=False,
    )
```

```python
import jax
import jax.numpy as jnp
from jax import lax
from jax.experimental import pallas as pl
from jax.sharding import Mesh
from jax.sharding import PartitionSpec as P

CUTS = ("zl", "core")
STEM = ("zh", "x", "y")
ROW_TILE = 256


def split_mesh(mesh):
    devices = mesh.devices.reshape(8, 2, 2, 4, 4)
    return Mesh(devices, CUTS + STEM)


def shift_pairs(count, step):
    return [(i, (i + step) % count) for i in range(count)]


def ring_gather(block, axis):
    count = lax.axis_size(axis)
    from_left = lax.ppermute(block, axis, shift_pairs(count, 1))
    from_right = lax.ppermute(block, axis, shift_pairs(count, -1))
    half = block.shape[-1] // 2
    far_a = lax.ppermute(from_left[..., :half], axis, shift_pairs(count, 1))
    far_b = lax.ppermute(from_right[..., half:], axis, shift_pairs(count, -1))
    far = jnp.concatenate([far_a, far_b], axis=-1)
    return [block, from_right, far, from_left]


def permute_columns(block, order):
    width = block.shape[-1]
    one_hot = (lax.broadcasted_iota(jnp.int32, (width, width), 0) == order[None, :]).astype(block.dtype)
    flat = block.reshape(-1, width)
    moved = jnp.dot(flat, one_hot, preferred_element_type=jnp.float32)
    return moved.astype(block.dtype).reshape(block.shape)


def contract_kernel(s_ref, b_ref, o_ref, out_ref):
    f32 = jnp.float32
    for t in range(s_ref.shape[0]):
        sr = s_ref[t, 0]
        si = s_ref[t, 1]
        br = b_ref[t, 0]
        bi = b_ref[t, 1]
        pr = jnp.dot(sr, br, preferred_element_type=f32) - jnp.dot(si, bi, preferred_element_type=f32)
        pi = jnp.dot(sr, bi, preferred_element_type=f32) + jnp.dot(si, br, preferred_element_type=f32)
        o_r = o_ref[t, :, 0, :].astype(f32)
        o_i = o_ref[t, :, 1, :].astype(f32)
        re = pr * o_r - pi * o_i
        im = pr * o_i + pi * o_r
        if t == 0:
            out_ref[0] = re
            out_ref[1] = im
        else:
            out_ref[0] += re
            out_ref[1] += im


def contract(stem_t, branch_t, open_t, column_block):
    slices, _, rows, depth = stem_t.shape
    width = branch_t.shape[-1]
    tile = min(ROW_TILE, rows)
    flops = slices * 8 * rows * depth * width
    moved = 2 * (stem_t.size + branch_t.size) + 2 * slices * 2 * rows * width + 4 * 2 * rows * width
    return pl.pallas_call(
        contract_kernel,
        out_shape=jax.ShapeDtypeStruct((2, rows, width), jnp.float32),
        grid=(rows // tile,),
        in_specs=[
            pl.BlockSpec((slices, 2, tile, depth), lambda i: (0, 0, i, 0)),
            pl.BlockSpec((slices, 2, depth, width), lambda i: (0, 0, 0, 0)),
            pl.BlockSpec((slices, tile, 2, width), lambda i: (0, i, 0, column_block)),
        ],
        out_specs=pl.BlockSpec((2, tile, width), lambda i: (0, i, 0)),
        cost_estimate=pl.CostEstimate(flops=flops, bytes_accessed=moved, transcendentals=0),
    )(stem_t, branch_t, open_t)


def halving_scatter(blocks, axis):
    count = lax.axis_size(axis)
    me = lax.axis_index(axis)
    shaped = blocks.reshape((2,) + (2,) * 3 + blocks.shape[2:])
    for bit_pos in range(3):
        along = 3 - bit_pos
        bit = (me >> bit_pos) & 1
        keep = lax.dynamic_index_in_dim(shaped, bit, along, keepdims=False)
        send = lax.dynamic_index_in_dim(shaped, 1 - bit, along, keepdims=False)
        pairs = [(i, i ^ (1 << bit_pos)) for i in range(count)]
        shaped = keep + lax.ppermute(send, axis, pairs)
    return shaped


def body(stem_tensor, branch_tensor, open_tensor, open_order):
    slice_count, row_count, _, width = stem_tensor.shape
    other_raw = lax.ppermute(branch_tensor, "zh", shift_pairs(2, 1))

    def permuted_of(shard):
        moved = jnp.stack([permute_columns(shard[t], open_order[t]) for t in range(slice_count)])
        return jnp.transpose(moved, (0, 2, 1, 3))

    permuted = permuted_of(branch_tensor)
    stem_t = jnp.transpose(stem_tensor, (0, 2, 1, 3))
    other_raw, stem_t = lax.optimization_barrier((other_raw, stem_t))
    other = permuted_of(other_raw)
    low = lax.axis_index("zh") == 0
    pair = jnp.where(low, jnp.stack([permuted, other], axis=2), jnp.stack([other, permuted], axis=2))
    plane = lax.axis_size("x") * lax.axis_size("y")
    copies = jnp.broadcast_to(pair[:, :, None], pair.shape[:2] + (plane,) + pair.shape[2:])
    halves = 2
    span = width // halves
    open_t = open_tensor
    zl_count = lax.axis_size("zl")
    block_rows = row_count // (zl_count * 2)
    core = lax.axis_index("core")
    results = []
    previous = None
    for h in range(halves):
        part = copies[..., h * span:(h + 1) * span]
        if previous is not None:
            part, previous = lax.optimization_barrier((part, previous))
        gathered = lax.all_to_all(part, ("x", "y"), 2, 4, tiled=True)
        previous = gathered
        branch_t = gathered.reshape(slice_count, 2, -1, span)
        local_sum = contract(stem_t, branch_t, open_t, h)
        shaped = local_sum.reshape(2, zl_count, 2, block_rows, span)
        mine = lax.dynamic_index_in_dim(shaped, core, 2, keepdims=False)
        theirs = lax.dynamic_index_in_dim(shaped, 1 - core, 2, keepdims=False)
        mine = mine + lax.ppermute(theirs, "core", shift_pairs(2, 1))
        results.append(halving_scatter(mine, "zl"))
    result = jnp.concatenate(results, axis=-1)
    return jnp.transpose(result, (1, 0, 2)).reshape(1, block_rows, 2, width)


def solution(mesh):
    fine = split_mesh(mesh)
    spec = P(CUTS, STEM, None, None)
    return jax.shard_map(
        body,
        mesh=fine,
        in_specs=(spec, spec, spec, P(CUTS, None)),
        out_specs=P(STEM, CUTS, None, None),
        check_vma=False,
    )
```
